512 devices in a mesh: rows: 32 (over x, y, core), cols: 16 (over z).
Axes of the slice: x: 4, y: 4, z: 16, core: 2. Of those that a mesh axis runs over, the one named last changes fastest.
Arguments:
- panel_t: float32 [256, 65536], P('cols', 'rows'), as said below
- trailing: float32 [65536, 4096], P('rows', 'cols'), may hold values from -6 to 6
- prev_lower_t: float32 [256, 65536], P('cols', 'rows'), may hold values from -6 to 6
- prev_upper: float32 [256, 4096], P(None, 'cols'), may hold values from -0.375 to 0.375
- leaf_picks: int32 [32, 256], P('rows'), may hold values from 0 to 2047, as said below
- merge_picks: int32 [31, 256], replicated, may hold values from 0 to 511, as said below
Outputs:
- lower_t: float32 [256, 65536], P('cols', 'rows')
- upper_left: float32 [256, 256], replicated
- upper_right: float32 [256, 4096], P(None, 'cols')
- updated: float32 [65536, 4096], P('rows', 'cols')
- gram: float32 [256, 256], P('cols')
The draws below stay inside these ranges and needn't reach their ends.
Inputs may be any that keep to these rules, and one draw needn't show every extreme that they name: `leaf_picks`: each row lists 256 different row numbers within the 2048 rows of one index of rows. `merge_picks`: each row lists 256 different positions in a stack of two candidate lists. `panel_t`: the rows of the panel at the pivots form a strictly diagonally dominant block.
All inputs are finite; a program needn't handle non-finite values.
Results may differ from the reference program's by a relative error of at most 0.0003.
Values sent between devices are 32-bit elements; how exact they have to be, the bound alone decides.
No kernel may reach another device: no remote copies, remote signals or barrier semaphores. Data moves between devices by JAX's collectives and lax.ppermute only.
A program may use at most 64 MiB of HBM per device.

```python
import math
import jax
import jax.numpy as jnp
from jax import lax

B = 256
ROWS_DEV = 2048
M = 65536
TRAIL = 4096
N_ROWS = 32


def forced_row(key, upper_bound, list_width):
    middle_values = jax.random.permutation(key, upper_bound - 2)[:list_width - 2].astype(jnp.int32) + 1
    end_values = jnp.array([0, upper_bound - 1], dtype=jnp.int32)
    joined = jnp.concatenate([middle_values, end_values])
    return jax.random.permutation(jax.random.fold_in(key, 7), joined)


def pick_table(key, row_count, upper_bound, list_width):
    key_list = jax.random.split(key, row_count)
    drawn_rows = jax.vmap(lambda subkey: jax.random.permutation(subkey, upper_bound)[:list_width].astype(jnp.int32))(key_list)
    return drawn_rows.at[0].set(forced_row(key_list[0], upper_bound, list_width))


def pick_lists(key):
    row_devices = M // ROWS_DEV
    leaves = pick_table(jax.random.fold_in(key, 101), row_devices, ROWS_DEV, B)
    merges = pick_table(jax.random.fold_in(key, 202), row_devices - 1, 2 * B, B)
    return (leaves, merges)


def trace_pivots_drawn(merge_picks, row_devices):
    list_width = merge_picks.shape[1]
    leaf_group = jnp.zeros((list_width,), jnp.int32)
    leaf_slot = jnp.arange(list_width, dtype=jnp.int32)
    levels = row_devices.bit_length() - 1
    for section in reversed(range(levels)):
        offset_rows = row_devices - (row_devices >> section)
        position = merge_picks[offset_rows + leaf_group, leaf_slot].astype(jnp.int32)
        right_side = (position >= list_width).astype(jnp.int32)
        leaf_group = 2 * leaf_group + right_side
        leaf_slot = position - list_width * right_side
    return (leaf_group, leaf_slot)


def draw_leaf_picks(key, part):
    return pick_lists(key)[0]


def draw_merge_picks(key, part):
    return pick_lists(key)[1]


def draw_panel_t(key, part):
    leaves, merges = pick_lists(key)
    row_devices = M // ROWS_DEV
    leaf_group, leaf_slot = trace_pivots_drawn(merges, row_devices)
    pivots = leaf_group * ROWS_DEV + leaves[leaf_group, leaf_slot]
    key_list = jax.random.split(jax.random.fold_in(key, 303), 6)
    position = jnp.arange(M, dtype=jnp.float32) / float(max(M - 1, 1))
    normal_part = jax.random.normal(key_list[0], (B, M), jnp.float32)
    row_ramp = 1.0 + 2.0 * position
    common_scale = 0.7
    block_mean = 0.6
    block_diagonal = 1.15
    spread = jnp.exp(jax.random.uniform(key_list[1], (M,), jnp.float32, 0.0, math.log(10.0)))
    common = jax.random.normal(key_list[2], (M,), jnp.float32) * common_scale
    column = 0.8 + 0.6 * jax.random.normal(key_list[3], (B,), jnp.float32)
    values = 0.08 * (spread * row_ramp)[None, :] * (normal_part + column[:, None] * common[None, :])
    wiggle = jax.random.uniform(key_list[4], (B, B), jnp.float32, -1.0, 1.0)
    pivot_scale = jnp.exp(jax.random.uniform(key_list[5], (B,), jnp.float32, 0.0, math.log(3.0)))
    identity = jnp.eye(B, dtype=jnp.float32)
    block = (block_mean + 0.5 * wiggle) * (1.0 / B) * (1.0 - identity) + block_diagonal * identity
    dominant = (pivot_scale[:, None] * block).T
    return values.at[:, pivots].set(dominant)


def level_of(stream_key, shape, cuts, smallest, high):
    gain = 1.0
    for dim, blocks in cuts:
        heights = jax.random.uniform(jax.random.fold_in(jax.random.fold_in(stream_key, 6), dim), (blocks,), jnp.float32, smallest / len(cuts), high / len(cuts))
        gain = gain * jnp.repeat(jnp.exp(heights), shape[dim] // blocks).reshape((-1,) + (1,) * (len(shape) - 1 - dim))
    return gain


def scatter_about(own_key, shape, scale, reach, pieces=(), kind=jnp.bfloat16):
    values = jax.random.normal(own_key, shape, jnp.float32) * scale
    if len(pieces) > 0:
        values = level_of(own_key, shape, pieces, -0.22, 0.18) * values
    return jnp.clip(values, min=-reach, max=reach).astype(kind)


def setup_inputs(seed: int = 0) -> dict:
    keys = jax.random.split(jax.random.key(seed), 7)
    panel_t = draw_panel_t(jax.random.fold_in(keys[6], 71), 0)
    trailing = scatter_about(keys[1], (M, TRAIL), 1.0, 6.0, ((0, 32), (1, 16)), jnp.float32)
    prev_lower_t = scatter_about(keys[2], (B, M), 1.0, 6.0, ((0, 16), (1, 32)), jnp.float32)
    prev_upper = scatter_about(keys[3], (B, TRAIL), B ** -0.5, 0.375, ((1, 16),), jnp.float32)
    leaf_picks = draw_leaf_picks(jax.random.fold_in(keys[6], 71), 0)
    merge_picks = draw_merge_picks(jax.random.fold_in(keys[6], 71), 0)
    return dict(panel_t=panel_t, trailing=trailing, prev_lower_t=prev_lower_t, prev_upper=prev_upper, leaf_picks=leaf_picks, merge_picks=merge_picks)


full_precision = lax.Precision.HIGHEST

def trace_pivots(merge_picks, row_devices):
    list_width = merge_picks.shape[1]
    leaf_group = jnp.zeros((list_width,), jnp.int32)
    leaf_slot = jnp.arange(list_width, dtype=jnp.int32)
    levels = row_devices.bit_length() - 1
    for section in reversed(range(levels)):
        offset_rows = row_devices - (row_devices >> section)
        position = merge_picks[offset_rows + leaf_group, leaf_slot].astype(jnp.int32)
        right_side = (position >= list_width).astype(jnp.int32)
        leaf_group = 2 * leaf_group + right_side
        leaf_slot = position - list_width * right_side
    return (leaf_group, leaf_slot)

def factor(matrix):
    order = matrix.shape[0]
    if order <= 32:
        reduced = matrix
        for column_index in range(order - 1):
            factors = reduced[column_index + 1:, column_index] / reduced[column_index, column_index]
            reduced = reduced.at[column_index + 1:, column_index + 1:].add(-factors[:, None] * reduced[column_index, column_index + 1:][None, :])
            reduced = reduced.at[column_index + 1:, column_index].set(factors)
        return (jnp.tril(reduced, -1) + jnp.eye(order, dtype=matrix.dtype), jnp.triu(reduced))
    middle_index = order // 2
    lower_head, upper_head = factor(matrix[:middle_index, :middle_index])
    upper_side = jax.scipy.linalg.solve_triangular(lower_head, matrix[:middle_index, middle_index:], lower=True, unit_diagonal=True)
    lower_side = jax.scipy.linalg.solve_triangular(upper_head, matrix[middle_index:, :middle_index].T, trans=1, lower=False).T
    schur_block = matrix[middle_index:, middle_index:] - jnp.dot(lower_side, upper_side, precision=full_precision)
    lower_tail, upper_tail = factor(schur_block)
    zero_upper = jnp.zeros((middle_index, order - middle_index), matrix.dtype)
    zero_lower = jnp.zeros((order - middle_index, middle_index), matrix.dtype)
    lower_full = jnp.concatenate([jnp.concatenate([lower_head, zero_upper], 1), jnp.concatenate([lower_side, lower_tail], 1)], 0)
    upper_full = jnp.concatenate([jnp.concatenate([upper_head, upper_side], 1), jnp.concatenate([zero_lower, upper_tail], 1)], 0)
    return (lower_full, upper_full)

def contract_first(left_side, right_side):
    return lax.dot_general(left_side, right_side, (((0,), (0,)), ((), ())), precision=full_precision)

def reference(panel_t, trailing, prev_lower_t, prev_upper, leaf_picks, merge_picks):
    leaf_group, leaf_slot = trace_pivots(merge_picks, N_ROWS)
    pivots = leaf_group * ROWS_DEV + leaf_picks[leaf_group, leaf_slot].astype(jnp.int32)
    pivot_block = panel_t[:, pivots].T
    lower_left, upper_left = factor(pivot_block)
    inverse = jax.scipy.linalg.solve_triangular(upper_left, jnp.eye(B, dtype=upper_left.dtype), lower=False)
    lower_t = jnp.dot(inverse.T, panel_t, precision=full_precision)
    middle_pivots = trailing[pivots] - contract_first(prev_lower_t[:, pivots], prev_upper)
    upper_right = jax.scipy.linalg.solve_triangular(lower_left, middle_pivots, lower=True, unit_diagonal=True)
    trail_blocks = trailing.reshape(N_ROWS, ROWS_DEV, TRAIL)
    prev_blocks = jnp.moveaxis(prev_lower_t.reshape(B, N_ROWS, ROWS_DEV), 1, 0)
    lower_blocks = jnp.moveaxis(lower_t.reshape(B, N_ROWS, ROWS_DEV), 1, 0)

    def update_block(operands):
        trail_rows, prev_rows, lower_rows = operands
        middle = trail_rows - contract_first(prev_rows, prev_upper)
        return middle - contract_first(lower_rows, upper_right)
    updated = lax.map(update_block, (trail_blocks, prev_blocks, lower_blocks)).reshape(M, TRAIL)
    gram = lax.dot_general(lower_t, lower_t, (((1,), (1,)), ((), ())), precision=full_precision) / M
    return (lower_t, upper_left, upper_right, updated, gram)
```

```python
import jax
import jax.numpy as jnp
from jax import lax
from jax.experimental import pallas as pl
from jax.experimental.pallas import tpu as pltpu
from jax.sharding import PartitionSpec as P

full_precision = lax.Precision.HIGHEST


def from_partner(shard, axis, apart):
    return lax.ppermute(shard, axis, [(i, i ^ 1 << apart) for i in range(lax.axis_size(axis))])


def trace_pivots(merge_picks, row_devices):
    list_width = merge_picks.shape[1]
    leaf_group = jnp.zeros((list_width,), jnp.int32)
    leaf_slot = jnp.arange(list_width, dtype=jnp.int32)
    levels = row_devices.bit_length() - 1
    for section in reversed(range(levels)):
        offset_rows = row_devices - (row_devices >> section)
        position = merge_picks[offset_rows + leaf_group, leaf_slot]
        right_side = (position >= list_width).astype(jnp.int32)
        leaf_group = 2 * leaf_group + right_side
        leaf_slot = position - list_width * right_side
    return (leaf_group, leaf_slot)


def product(left_side, right_side):
    return jnp.dot(left_side, right_side, precision=full_precision)


def unit_lower_inverse(lower):
    order = lower.shape[0]
    identity = jnp.eye(order, dtype=jnp.float32)
    power = identity - lower
    result = identity + power
    covered = 1
    while covered < order - 1:
        power = product(power, power)
        result = product(result, identity + power)
        covered = 2 * covered + 1
    return result


def upper_inverse(upper):
    diagonal = jnp.diagonal(upper)
    scaled = upper / diagonal[:, None]
    unit_inverse = unit_lower_inverse(scaled.T).T
    return unit_inverse / diagonal[None, :]


def elimination_kernel(matrix_ref, reduced_ref):
    order = matrix_ref.shape[0]
    reduced_ref[...] = matrix_ref[...]
    phase = 32
    for first_row in range(0, order - 1, phase):
        first_col = (first_row // 128) * 128
        height = order - first_row
        width = order - first_col
        row_index = lax.broadcasted_iota(jnp.int32, (height, width), 0) + first_row
        col_index = lax.broadcasted_iota(jnp.int32, (height, width), 1) + first_col

        def step(column_index, carry):
            window = reduced_ref[first_row:, first_col:]
            pivot_line = reduced_ref[pl.ds(column_index, 1), :][:, first_col:]
            on_column = col_index == column_index
            pivot_column = jnp.sum(jnp.where(on_column, window, 0.0), axis=1, keepdims=True)
            pivot_value = jnp.sum(
                jnp.where(on_column[0:1], pivot_line, 0.0), axis=1, keepdims=True
            )
            factors = pivot_column / pivot_value
            below = row_index > column_index
            window = jnp.where(
                below & (col_index > column_index), window - factors * pivot_line, window
            )
            window = jnp.where(below & on_column, factors, window)
            reduced_ref[first_row:, first_col:] = window
            return carry

        lax.fori_loop(first_row, min(first_row + phase, order - 1), step, 0)


def factor(matrix):
    order = matrix.shape[0]
    reduced = pl.pallas_call(
        elimination_kernel,
        out_shape=jax.ShapeDtypeStruct(matrix.shape, matrix.dtype),
    )(matrix)
    lower = jnp.tril(reduced, -1) + jnp.eye(order, dtype=matrix.dtype)
    return (lower, jnp.triu(reduced))


def contract_first(left_side, right_side):
    return lax.dot_general(
        left_side, right_side, (((0,), (0,)), ((), ())), precision=full_precision
    )


def contract_second(left_side, right_side):
    return lax.dot_general(
        left_side, right_side, (((1,), (1,)), ((), ())), precision=full_precision
    )


def body(panel_t, trailing, prev_lower_t, prev_upper, leaf_picks, merge_picks):
    slab_rows = panel_t.shape[0]
    rows_here = panel_t.shape[1]
    row_devices = lax.axis_size("rows")
    own_row = lax.axis_index("rows")
    own_column = lax.axis_index("cols")
    leaf_group, leaf_slot = trace_pivots(merge_picks, row_devices)
    owner_mask = leaf_group == own_row
    local_rows = jnp.take(leaf_picks[0], leaf_slot)
    middle = trailing
    middle = middle - contract_first(
        lax.all_gather(prev_lower_t, "cols", axis=0, tiled=True), prev_upper
    )
    panel_full = lax.all_gather(panel_t, "cols", axis=0, tiled=True)
    middle, panel_full = (middle, panel_full)
    candidates = jnp.take(panel_t, leaf_picks[0], axis=1)
    levels = row_devices.bit_length() - 1
    for section in range(levels):
        partner = from_partner(candidates, "rows", section)
        upper_half = own_row >> section & 1
        stacked = jnp.where(
            upper_half == 0,
            jnp.concatenate([candidates, partner], 1),
            jnp.concatenate([partner, candidates], 1),
        )
        merge_index = row_devices - (row_devices >> section) + (own_row >> section + 1)
        selection = lax.dynamic_index_in_dim(merge_picks, merge_index, 0, keepdims=False)
        candidates = jnp.take(stacked, selection, axis=1)
    block_t = lax.all_gather(candidates, "cols", axis=0, tiled=True)
    lower_left, upper_left = factor(block_t.T)
    inverse = upper_inverse(upper_left)
    chosen_rows = jnp.take(middle, local_rows, axis=0)
    pivot_trailing = lax.psum(jnp.where(owner_mask[:, None], chosen_rows, 0.0), "rows")
    upper_right = product(unit_lower_inverse(lower_left), pivot_trailing)
    lower_full = jnp.dot(inverse.T, panel_full, precision=full_precision)
    lower_tile = lax.dynamic_slice_in_dim(lower_full, own_column * slab_rows, slab_rows, 0)
    updated = middle - contract_first(lower_full, upper_right)
    gram_rows = contract_second(lower_tile, lower_full)
    gram = lax.psum(gram_rows, "rows") / (rows_here * row_devices)
    return (lower_tile, upper_left, upper_right, updated, gram)


def solution(mesh):
    return jax.shard_map(
        body,
        mesh=mesh,
        in_specs=(
            P("cols", "rows"),
            P("rows", "cols"),
            P("cols", "rows"),
            P(None, "cols"),
            P("rows", None),
            P(),
        ),
        out_specs=(P("cols", "rows"), P(), P(None, "cols"), P("rows", "cols"), P("cols", None)),
        check_vma=False,
    )
```

```python
import jax
import jax.numpy as jnp
from jax import lax
from jax.experimental import pallas as pl
from jax.experimental.pallas import tpu as pltpu
from jax.sharding import PartitionSpec as P

full_precision = lax.Precision.HIGHEST


def from_partner(shard, axis, apart):
    return lax.ppermute(shard, axis, [(i, i ^ 1 << apart) for i in range(lax.axis_size(axis))])


def trace_pivots(merge_picks, row_devices):
    list_width = merge_picks.shape[1]
    leaf_group = jnp.zeros((list_width,), jnp.int32)
    leaf_slot = jnp.arange(list_width, dtype=jnp.int32)
    levels = row_devices.bit_length() - 1
    for section in reversed(range(levels)):
        offset_rows = row_devices - (row_devices >> section)
        position = merge_picks[offset_rows + leaf_group, leaf_slot]
        right_side = (position >= list_width).astype(jnp.int32)
        leaf_group = 2 * leaf_group + right_side
        leaf_slot = position - list_width * right_side
    return (leaf_group, leaf_slot)


def product(left_side, right_side):
    return jnp.dot(left_side, right_side, precision=full_precision)


def unit_lower_inverse(lower):
    order = lower.shape[0]
    identity = jnp.eye(order, dtype=jnp.float32)
    power = identity - lower
    result = identity + power
    covered = 1
    while covered < order - 1:
        power = product(power, power)
        result = product(result, identity + power)
        covered = 2 * covered + 1
    return result


def upper_inverse(upper):
    diagonal = jnp.diagonal(upper)
    scaled = upper / diagonal[:, None]
    unit_inverse = unit_lower_inverse(scaled.T).T
    return unit_inverse / diagonal[None, :]


def elimination_kernel(matrix_ref, reduced_ref):
    order = matrix_ref.shape[0]
    reduced_ref[...] = matrix_ref[...]
    phase = 32
    for first_row in range(0, order - 1, phase):
        first_col = (first_row // 128) * 128
        height = order - first_row
        width = order - first_col
        row_index = lax.broadcasted_iota(jnp.int32, (height, width), 0) + first_row
        col_index = lax.broadcasted_iota(jnp.int32, (height, width), 1) + first_col

        def step(column_index, carry):
            window = reduced_ref[first_row:, first_col:]
            pivot_line = reduced_ref[pl.ds(column_index, 1), :][:, first_col:]
            on_column = col_index == column_index
            pivot_column = jnp.sum(jnp.where(on_column, window, 0.0), axis=1, keepdims=True)
            pivot_value = jnp.sum(
                jnp.where(on_column[0:1], pivot_line, 0.0), axis=1, keepdims=True
            )
            factors = pivot_column / pivot_value
            below = row_index > column_index
            window = jnp.where(
                below & (col_index > column_index), window - factors * pivot_line, window
            )
            window = jnp.where(below & on_column, factors, window)
            reduced_ref[first_row:, first_col:] = window
            return carry

        lax.fori_loop(first_row, min(first_row + phase, order - 1), step, 0)


def factor(matrix):
    order = matrix.shape[0]
    reduced = pl.pallas_call(
        elimination_kernel,
        out_shape=jax.ShapeDtypeStruct(matrix.shape, matrix.dtype),
    )(matrix)
    lower = jnp.tril(reduced, -1) + jnp.eye(order, dtype=matrix.dtype)
    return (lower, jnp.triu(reduced))


def contract_first(left_side, right_side):
    return lax.dot_general(
        left_side, right_side, (((0,), (0,)), ((), ())), precision=full_precision
    )


def contract_second(left_side, right_side):
    return lax.dot_general(
        left_side, right_side, (((1,), (1,)), ((), ())), precision=full_precision
    )


def butterfly_sum(value, axis):
    levels = lax.axis_size(axis).bit_length() - 1
    for section in range(levels):
        value = value + from_partner(value, axis, section)
    return value


def body(panel_t, trailing, prev_lower_t, prev_upper, leaf_picks, merge_picks):
    slab_rows = panel_t.shape[0]
    rows_here = panel_t.shape[1]
    order = merge_picks.shape[1]
    row_devices = lax.axis_size("rows")
    own_row = lax.axis_index("rows")
    own_column = lax.axis_index("cols")
    leaf_group, leaf_slot = trace_pivots(merge_picks, row_devices)
    owner_mask = leaf_group == own_row
    local_rows = jnp.take(leaf_picks[0], leaf_slot)
    own_trailing = jnp.take(trailing, local_rows, axis=0)
    own_columns = jnp.take(jnp.concatenate([panel_t, prev_lower_t], 0), local_rows, axis=1)
    own_pivots = jnp.concatenate([own_trailing, own_columns.T], 1)
    pivot_data = butterfly_sum(jnp.where(owner_mask[:, None], own_pivots, 0.0), "rows")
    pivot_trailing = pivot_data[:, : own_trailing.shape[1]]
    pivot_columns = lax.all_gather(
        pivot_data[:, own_trailing.shape[1] :].T, "cols", axis=0, tiled=False
    )
    block_t = pivot_columns[:, :slab_rows].reshape(order, order)
    prev_pivots = pivot_columns[:, slab_rows:].reshape(order, order)
    middle_pivots = pivot_trailing - contract_first(prev_pivots, prev_upper)
    middle = trailing - contract_first(
        lax.all_gather(prev_lower_t, "cols", axis=0, tiled=True), prev_upper
    )
    panel_full = lax.all_gather(panel_t, "cols", axis=0, tiled=True)
    lower_left, upper_left = factor(block_t.T)
    inverse = upper_inverse(upper_left)
    upper_right = product(unit_lower_inverse(lower_left), middle_pivots)
    lower_full = jnp.dot(inverse.T, panel_full, precision=full_precision)
    lower_tile = lax.dynamic_slice_in_dim(lower_full, own_column * slab_rows, slab_rows, 0)
    updated = middle - contract_first(lower_full, upper_right)
    gram_rows = contract_second(lower_tile, lower_full)
    gram = butterfly_sum(gram_rows, "rows") / (rows_here * row_devices)
    return (lower_tile, upper_left, upper_right, updated, gram)


def solution(mesh):
    return jax.shard_map(
        body,
        mesh=mesh,
        in_specs=(
            P("cols", "rows"),
            P("rows", "cols"),
            P("cols", "rows"),
            P(None, "cols"),
            P("rows", None),
            P(),
        ),
        out_specs=(P("cols", "rows"), P(), P(None, "cols"), P("rows", "cols"), P("cols", None)),
        check_vma=False,
    )
```

```python
import jax
import jax.numpy as jnp
from jax import lax
from jax.experimental import pallas as pl
from jax.experimental.pallas import tpu as pltpu
from jax.sharding import PartitionSpec as P

full_precision = lax.Precision.HIGHEST


def from_partner(shard, axis, apart):
    return lax.ppermute(shard, axis, [(i, i ^ 1 << apart) for i in range(lax.axis_size(axis))])


def trace_pivots(merge_picks, row_devices):
    list_width = merge_picks.shape[1]
    leaf_group = jnp.zeros((list_width,), jnp.int32)
    leaf_slot = jnp.arange(list_width, dtype=jnp.int32)
    levels = row_devices.bit_length() - 1
    for section in reversed(range(levels)):
        offset_rows = row_devices - (row_devices >> section)
        position = merge_picks[offset_rows + leaf_group, leaf_slot]
        right_side = (position >= list_width).astype(jnp.int32)
        leaf_group = 2 * leaf_group + right_side
        leaf_slot = position - list_width * right_side
    return (leaf_group, leaf_slot)


def product(left_side, right_side):
    return jnp.dot(left_side, right_side, precision=full_precision)


def unit_lower_inverse(lower):
    order = lower.shape[0]
    identity = jnp.eye(order, dtype=jnp.float32)
    power = identity - lower
    result = identity + power
    covered = 1
    while covered < order - 1:
        power = product(power, power)
        result = product(result, identity + power)
        covered = 2 * covered + 1
    return result


def upper_inverse(upper):
    diagonal = jnp.diagonal(upper)
    scaled = upper / diagonal[:, None]
    unit_inverse = unit_lower_inverse(scaled.T).T
    return unit_inverse / diagonal[None, :]


def elimination_kernel(matrix_ref, reduced_ref):
    order = matrix_ref.shape[0]
    reduced_ref[...] = matrix_ref[...]
    phase = 32
    for first_row in range(0, order - 1, phase):
        first_col = (first_row // 128) * 128
        height = order - first_row
        width = order - first_col
        row_index = lax.broadcasted_iota(jnp.int32, (height, width), 0) + first_row
        col_index = lax.broadcasted_iota(jnp.int32, (height, width), 1) + first_col

        def step(column_index, carry):
            window = reduced_ref[first_row:, first_col:]
            pivot_line = reduced_ref[pl.ds(column_index, 1), :][:, first_col:]
            on_column = col_index == column_index
            pivot_column = jnp.sum(jnp.where(on_column, window, 0.0), axis=1, keepdims=True)
            pivot_value = jnp.sum(
                jnp.where(on_column[0:1], pivot_line, 0.0), axis=1, keepdims=True
            )
            factors = pivot_column / pivot_value
            below = row_index > column_index
            window = jnp.where(
                below & (col_index > column_index), window - factors * pivot_line, window
            )
            window = jnp.where(below & on_column, factors, window)
            reduced_ref[first_row:, first_col:] = window
            return carry

        lax.fori_loop(first_row, min(first_row + phase, order - 1), step, 0)


def factor(matrix):
    order = matrix.shape[0]
    reduced = pl.pallas_call(
        elimination_kernel,
        out_shape=jax.ShapeDtypeStruct(matrix.shape, matrix.dtype),
    )(matrix)
    lower = jnp.tril(reduced, -1) + jnp.eye(order, dtype=matrix.dtype)
    return (lower, jnp.triu(reduced))


def contract_first(left_side, right_side):
    return lax.dot_general(
        left_side, right_side, (((0,), (0,)), ((), ())), precision=full_precision
    )


def contract_second(left_side, right_side):
    return lax.dot_general(
        left_side, right_side, (((1,), (1,)), ((), ())), precision=full_precision
    )


def butterfly_sum(value, axis):
    levels = lax.axis_size(axis).bit_length() - 1
    for section in range(levels):
        value = value + from_partner(value, axis, section)
    return value


def butterfly_gather(value, axis):
    levels = lax.axis_size(axis).bit_length() - 1
    own = lax.axis_index(axis)
    value = value[None]
    for section in range(levels):
        partner = from_partner(value, axis, section)
        value = jnp.where(
            own >> section & 1 == 0,
            jnp.concatenate([value, partner], 0),
            jnp.concatenate([partner, value], 0),
        )
    return value


def body(panel_t, trailing, prev_lower_t, prev_upper, leaf_picks, merge_picks):
    slab_rows = panel_t.shape[0]
    rows_here = panel_t.shape[1]
    order = merge_picks.shape[1]
    row_devices = lax.axis_size("rows")
    own_row = lax.axis_index("rows")
    own_column = lax.axis_index("cols")
    leaf_group, leaf_slot = trace_pivots(merge_picks, row_devices)
    owner_mask = leaf_group == own_row
    local_rows = jnp.take(leaf_picks[0], leaf_slot)
    own_columns = jnp.take(jnp.concatenate([panel_t, prev_lower_t], 0), local_rows, axis=1)
    pivot_part = butterfly_sum(jnp.where(owner_mask[None, :], own_columns, 0.0), "rows")
    pivot_columns = butterfly_gather(pivot_part, "cols")
    block_t = pivot_columns[:, :slab_rows].reshape(order, order)
    prev_pivots = pivot_columns[:, slab_rows:].reshape(order, order)
    own_trailing = jnp.take(trailing, local_rows, axis=0)
    pivot_trailing = butterfly_sum(jnp.where(owner_mask[:, None], own_trailing, 0.0), "rows")
    middle_pivots = pivot_trailing - contract_first(prev_pivots, prev_upper)
    middle = trailing - contract_first(
        lax.all_gather(prev_lower_t, "cols", axis=0, tiled=True), prev_upper
    )
    panel_full = lax.all_gather(panel_t, "cols", axis=0, tiled=True)
    lower_left, upper_left = factor(block_t.T)
    inverse = upper_inverse(upper_left)
    upper_right = product(unit_lower_inverse(lower_left), middle_pivots)
    lower_full = jnp.dot(inverse.T, panel_full, precision=full_precision)
    lower_tile = lax.dynamic_slice_in_dim(lower_full, own_column * slab_rows, slab_rows, 0)
    updated = middle - contract_first(lower_full, upper_right)
    gram_rows = contract_second(lower_tile, lower_full)
    gram = butterfly_sum(gram_rows, "rows") / (rows_here * row_devices)
    return (lower_tile, upper_left, upper_right, updated, gram)


def solution(mesh):
    return jax.shard_map(
        body,
        mesh=mesh,
        in_specs=(
            P("cols", "rows"),
            P("rows", "cols"),
            P("cols", "rows"),
            P(None, "cols"),
            P("rows", None),
            P(),
        ),
        out_specs=(P("cols", "rows"), P(), P(None, "cols"), P("rows", "cols"), P("cols", None)),
        check_vma=False,
    )
```

```python
import jax
import jax.numpy as jnp
from jax import lax
from jax.experimental import pallas as pl
from jax.experimental.pallas import tpu as pltpu
from jax.sharding import PartitionSpec as P

full_precision = lax.Precision.HIGHEST


def from_partner(shard, axis, apart):
    return lax.ppermute(shard, axis, [(i, i ^ 1 << apart) for i in range(lax.axis_size(axis))])


def trace_pivots(merge_picks, row_devices):
    list_width = merge_picks.shape[1]
    leaf_group = jnp.zeros((list_width,), jnp.int32)
    leaf_slot = jnp.arange(list_width, dtype=jnp.int32)
    levels = row_devices.bit_length() - 1
    for section in reversed(range(levels)):
        offset_rows = row_devices - (row_devices >> section)
        position = merge_picks[offset_rows + leaf_group, leaf_slot]
        right_side = (position >= list_width).astype(jnp.int32)
        leaf_group = 2 * leaf_group + right_side
        leaf_slot = position - list_width * right_side
    return (leaf_group, leaf_slot)


def product(left_side, right_side):
    return jnp.dot(left_side, right_side, precision=full_precision)


def unit_lower_inverse(lower):
    order = lower.shape[0]
    identity = jnp.eye(order, dtype=jnp.float32)
    power = identity - lower
    result = identity + power
    covered = 1
    while covered < order - 1:
        power = product(power, power)
        result = product(result, identity + power)
        covered = 2 * covered + 1
    return result


def upper_inverse(upper):
    diagonal = jnp.diagonal(upper)
    scaled = upper / diagonal[:, None]
    unit_inverse = unit_lower_inverse(scaled.T).T
    return unit_inverse / diagonal[None, :]


def elimination_kernel(matrix_ref, reduced_ref):
    order = matrix_ref.shape[0]
    reduced_ref[...] = matrix_ref[...]
    phase = 64
    for first_row in range(0, order - 1, phase):
        first_col = (first_row // 128) * 128
        height = order - first_row
        width = order - first_col
        row_index = lax.broadcasted_iota(jnp.int32, (height, width), 0) + first_row
        col_index = lax.broadcasted_iota(jnp.int32, (height, width), 1) + first_col

        def step(column_index, carry):
            window = reduced_ref[first_row:, first_col:]
            pivot_line = reduced_ref[pl.ds(column_index, 1), :][:, first_col:]
            on_column = col_index == column_index
            pivot_column = jnp.sum(jnp.where(on_column, window, 0.0), axis=1, keepdims=True)
            pivot_value = jnp.sum(
                jnp.where(on_column[0:1], pivot_line, 0.0), axis=1, keepdims=True
            )
            factors = pivot_column / pivot_value
            below = row_index > column_index
            window = jnp.where(
                below & (col_index > column_index), window - factors * pivot_line, window
            )
            window = jnp.where(below & on_column, factors, window)
            reduced_ref[first_row:, first_col:] = window
            return carry

        lax.fori_loop(first_row, min(first_row + phase, order - 1), step, 0)


def factor(matrix):
    order = matrix.shape[0]
    reduced = pl.pallas_call(
        elimination_kernel,
        out_shape=jax.ShapeDtypeStruct(matrix.shape, matrix.dtype),
    )(matrix)
    lower = jnp.tril(reduced, -1) + jnp.eye(order, dtype=matrix.dtype)
    return (lower, jnp.triu(reduced))


def contract_first(left_side, right_side):
    return lax.dot_general(
        left_side, right_side, (((0,), (0,)), ((), ())), precision=full_precision
    )


def contract_second(left_side, right_side):
    return lax.dot_general(
        left_side, right_side, (((1,), (1,)), ((), ())), precision=full_precision
    )


def butterfly_sum(value, axis):
    levels = lax.axis_size(axis).bit_length() - 1
    for section in range(levels):
        value = value + from_partner(value, axis, section)
    return value


def digit_exchange(value, axis, shift, width):
    size = lax.axis_size(axis)
    digit = lax.axis_index(axis) >> shift & (1 << width) - 1
    received = [value]
    for offset in range(1, 1 << width):
        pairs = [(i, i ^ offset << shift) for i in range(size)]
        received.append(lax.ppermute(value, axis, pairs))
    stacked = jnp.stack(received)
    return [
        lax.dynamic_index_in_dim(stacked, position ^ digit, 0, keepdims=False)
        for position in range(1 << width)
    ]


def digit_plan(size):
    plan = []
    shift = 0
    if size.bit_length() % 2 == 0:
        plan.append((0, 1))
        shift = 1
    while 1 << shift < size:
        plan.append((shift, 2))
        shift += 2
    return plan


def exchange_sum(value, axis):
    for shift, width in digit_plan(lax.axis_size(axis)):
        parts = digit_exchange(value, axis, shift, width)
        total = parts[0]
        for part in parts[1:]:
            total = total + part
        value = total
    return value


def exchange_gather(value, axis):
    value = value[None]
    for shift, width in digit_plan(lax.axis_size(axis)):
        value = jnp.concatenate(digit_exchange(value, axis, shift, width), 0)
    return value


def body(panel_t, trailing, prev_lower_t, prev_upper, leaf_picks, merge_picks):
    slab_rows = panel_t.shape[0]
    rows_here = panel_t.shape[1]
    order = merge_picks.shape[1]
    row_devices = lax.axis_size("rows")
    own_row = lax.axis_index("rows")
    own_column = lax.axis_index("cols")
    leaf_group, leaf_slot = trace_pivots(merge_picks, row_devices)
    owner_mask = leaf_group == own_row
    local_rows = jnp.take(leaf_picks[0], leaf_slot)
    own_columns = jnp.take(jnp.concatenate([panel_t, prev_lower_t], 0), local_rows, axis=1)
    pivot_part = exchange_sum(jnp.where(owner_mask[None, :], own_columns, 0.0), "rows")
    pivot_columns = exchange_gather(pivot_part, "cols")
    own_trailing = jnp.take(trailing, local_rows, axis=0)
    own_trailing = jnp.where(owner_mask[:, None], own_trailing, 0.0)
    own_trailing, pivot_columns = lax.optimization_barrier((own_trailing, pivot_columns))
    pivot_trailing = exchange_sum(own_trailing, "rows")
    block_t = pivot_columns[:, :slab_rows].reshape(order, order)
    prev_pivots = pivot_columns[:, slab_rows:].reshape(order, order)
    middle_pivots = pivot_trailing - contract_first(prev_pivots, prev_upper)
    middle = trailing - contract_first(
        lax.all_gather(prev_lower_t, "cols", axis=0, tiled=True), prev_upper
    )
    panel_full = lax.all_gather(panel_t, "cols", axis=0, tiled=True)
    lower_left, upper_left = factor(block_t.T)
    inverse = upper_inverse(upper_left)
    upper_right = product(unit_lower_inverse(lower_left), middle_pivots)
    lower_full = jnp.dot(inverse.T, panel_full, precision=full_precision)
    lower_tile = lax.dynamic_slice_in_dim(lower_full, own_column * slab_rows, slab_rows, 0)
    updated = middle - contract_first(lower_full, upper_right)
    gram_rows = contract_second(lower_tile, lower_full)
    gram = butterfly_sum(gram_rows, "rows") / (rows_here * row_devices)
    return (lower_tile, upper_left, upper_right, updated, gram)


def solution(mesh):
    return jax.shard_map(
        body,
        mesh=mesh,
        in_specs=(
            P("cols", "rows"),
            P("rows", "cols"),
            P("cols", "rows"),
            P(None, "cols"),
            P("rows", None),
            P(),
        ),
        out_specs=(P("cols", "rows"), P(), P(None, "cols"), P("rows", "cols"), P("cols", None)),
        check_vma=False,
    )
```

```python
import jax
import jax.numpy as jnp
from jax import lax
from jax.experimental import pallas as pl
from jax.experimental.pallas import tpu as pltpu
from jax.sharding import PartitionSpec as P

full_precision = lax.Precision.HIGHEST


def from_partner(shard, axis, apart):
    return lax.ppermute(shard, axis, [(i, i ^ 1 << apart) for i in range(lax.axis_size(axis))])


def trace_pivots(merge_picks, row_devices):
    list_width = merge_picks.shape[1]
    leaf_group = jnp.zeros((list_width,), jnp.int32)
    leaf_slot = jnp.arange(list_width, dtype=jnp.int32)
    levels = row_devices.bit_length() - 1
    for section in reversed(range(levels)):
        offset_rows = row_devices - (row_devices >> section)
        position = merge_picks[offset_rows + leaf_group, leaf_slot]
        right_side = (position >= list_width).astype(jnp.int32)
        leaf_group = 2 * leaf_group + right_side
        leaf_slot = position - list_width * right_side
    return (leaf_group, leaf_slot)


def product(left_side, right_side):
    return jnp.dot(left_side, right_side, precision=full_precision)


def unit_lower_inverse(lower):
    order = lower.shape[0]
    identity = jnp.eye(order, dtype=jnp.float32)
    power = identity - lower
    result = identity + power
    covered = 1
    while covered < order - 1:
        power = product(power, power)
        result = product(result, identity + power)
        covered = 2 * covered + 1
    return result


def upper_inverse(upper):
    diagonal = jnp.diagonal(upper)
    scaled = upper / diagonal[:, None]
    unit_inverse = unit_lower_inverse(scaled.T).T
    return unit_inverse / diagonal[None, :]


def elimination_kernel(matrix_ref, reduced_ref):
    order = matrix_ref.shape[0]
    reduced_ref[...] = matrix_ref[...]
    phase = 64
    for first_row in range(0, order - 1, phase):
        first_col = (first_row // 128) * 128
        height = order - first_row
        width = order - first_col
        row_index = lax.broadcasted_iota(jnp.int32, (height, width), 0) + first_row
        col_index = lax.broadcasted_iota(jnp.int32, (height, width), 1) + first_col

        def step(column_index, carry):
            window = reduced_ref[first_row:, first_col:]
            pivot_line = reduced_ref[pl.ds(column_index, 1), :][:, first_col:]
            on_column = col_index == column_index
            pivot_column = jnp.sum(jnp.where(on_column, window, 0.0), axis=1, keepdims=True)
            pivot_value = jnp.sum(
                jnp.where(on_column[0:1], pivot_line, 0.0), axis=1, keepdims=True
            )
            factors = pivot_column / pivot_value
            below = row_index > column_index
            window = jnp.where(
                below & (col_index > column_index), window - factors * pivot_line, window
            )
            window = jnp.where(below & on_column, factors, window)
            reduced_ref[first_row:, first_col:] = window
            return carry

        lax.fori_loop(first_row, min(first_row + phase, order - 1), step, 0)


def factor(matrix):
    order = matrix.shape[0]
    reduced = pl.pallas_call(
        elimination_kernel,
        out_shape=jax.ShapeDtypeStruct(matrix.shape, matrix.dtype),
    )(matrix)
    lower = jnp.tril(reduced, -1) + jnp.eye(order, dtype=matrix.dtype)
    return (lower, jnp.triu(reduced))


def contract_first(left_side, right_side):
    return lax.dot_general(
        left_side, right_side, (((0,), (0,)), ((), ())), precision=full_precision
    )


def contract_second(left_side, right_side):
    return lax.dot_general(
        left_side, right_side, (((1,), (1,)), ((), ())), precision=full_precision
    )


def butterfly_sum(value, axis):
    levels = lax.axis_size(axis).bit_length() - 1
    for section in range(levels):
        value = value + from_partner(value, axis, section)
    return value


def body(panel_t, trailing, prev_lower_t, prev_upper, leaf_picks, merge_picks):
    slab_rows = panel_t.shape[0]
    rows_here = panel_t.shape[1]
    order = merge_picks.shape[1]
    row_devices = lax.axis_size("rows")
    own_row = lax.axis_index("rows")
    own_column = lax.axis_index("cols")
    leaf_group, leaf_slot = trace_pivots(merge_picks, row_devices)
    owner_mask = leaf_group == own_row
    local_rows = jnp.take(leaf_picks[0], leaf_slot)
    own_columns = jnp.take(jnp.concatenate([panel_t, prev_lower_t], 0), local_rows, axis=1)
    pivot_part = butterfly_sum(jnp.where(owner_mask[None, :], own_columns, 0.0), "rows")
    pivot_columns = lax.all_gather(pivot_part, "cols", axis=0, tiled=False)
    own_trailing = jnp.take(trailing, local_rows, axis=0)
    own_trailing = jnp.where(owner_mask[:, None], own_trailing, 0.0)
    own_trailing, pivot_columns = lax.optimization_barrier((own_trailing, pivot_columns))
    pivot_trailing = butterfly_sum(own_trailing, "rows")
    block_t = pivot_columns[:, :slab_rows].reshape(order, order)
    prev_pivots = pivot_columns[:, slab_rows:].reshape(order, order)
    middle_pivots = pivot_trailing - contract_first(prev_pivots, prev_upper)
    middle = trailing - contract_first(
        lax.all_gather(prev_lower_t, "cols", axis=0, tiled=True), prev_upper
    )
    panel_full = lax.all_gather(panel_t, "cols", axis=0, tiled=True)
    panel_gram = butterfly_sum(contract_second(panel_full, panel_full), "rows")
    lower_left, upper_left = factor(block_t.T)
    inverse = upper_inverse(upper_left)
    upper_right = product(unit_lower_inverse(lower_left), middle_pivots)
    lower_full = jnp.dot(inverse.T, panel_full, precision=full_precision)
    lower_tile = lax.dynamic_slice_in_dim(lower_full, own_column * slab_rows, slab_rows, 0)
    updated = middle - contract_first(lower_full, upper_right)
    inverse_tile = lax.dynamic_slice_in_dim(inverse, own_column * slab_rows, slab_rows, 1)
    gram_rows = contract_first(inverse_tile, product(panel_gram, inverse))
    gram = gram_rows / (rows_here * row_devices)
    return (lower_tile, upper_left, upper_right, updated, gram)


def solution(mesh):
    return jax.shard_map(
        body,
        mesh=mesh,
        in_specs=(
            P("cols", "rows"),
            P("rows", "cols"),
            P("cols", "rows"),
            P(None, "cols"),
            P("rows", None),
            P(),
        ),
        out_specs=(P("cols", "rows"), P(), P(None, "cols"), P("rows", "cols"), P("cols", None)),
        check_vma=False,
    )
```

```python
import jax
import jax.numpy as jnp
from jax import lax
from jax.experimental import pallas as pl
from jax.experimental.pallas import tpu as pltpu
from jax.sharding import PartitionSpec as P

full_precision = lax.Precision.HIGHEST


def from_partner(shard, axis, apart):
    return lax.ppermute(shard, axis, [(i, i ^ 1 << apart) for i in range(lax.axis_size(axis))])


def lookup(table, group, slot):
    width = table.shape[1]
    slot_hit = slot[:, None] == lax.broadcasted_iota(jnp.int32, (slot.shape[0], width), 1)
    chosen = jnp.zeros((slot.shape[0], width), table.dtype)
    for index in range(table.shape[0]):
        chosen = jnp.where((group == index)[:, None], table[index][None, :], chosen)
    return jnp.sum(jnp.where(slot_hit, chosen, 0), axis=1)


def trace_pivots(merge_picks, row_devices):
    list_width = merge_picks.shape[1]
    leaf_group = jnp.zeros((list_width,), jnp.int32)
    leaf_slot = jnp.arange(list_width, dtype=jnp.int32)
    levels = row_devices.bit_length() - 1
    for section in reversed(range(levels)):
        offset_rows = row_devices - (row_devices >> section)
        groups = 1 << levels - 1 - section
        position = lookup(merge_picks[offset_rows : offset_rows + groups], leaf_group, leaf_slot)
        right_side = (position >= list_width).astype(jnp.int32)
        leaf_group = 2 * leaf_group + right_side
        leaf_slot = position - list_width * right_side
    return (leaf_group, leaf_slot)


def product(left_side, right_side):
    return jnp.dot(left_side, right_side, precision=full_precision)


def unit_lower_inverse(lower):
    order = lower.shape[0]
    identity = jnp.eye(order, dtype=jnp.float32)
    power = identity - lower
    result = identity + power
    covered = 1
    while covered < order - 1:
        power = product(power, power)
        result = product(result, identity + power)
        covered = 2 * covered + 1
    return result


def upper_inverse(upper):
    diagonal = jnp.diagonal(upper)
    scaled = upper / diagonal[:, None]
    unit_inverse = unit_lower_inverse(scaled.T).T
    return unit_inverse / diagonal[None, :]


def elimination_kernel(matrix_ref, reduced_ref):
    order = matrix_ref.shape[0]
    reduced_ref[...] = matrix_ref[...]
    phase = 32
    for first_row in range(0, order - 1, phase):
        first_col = (first_row // 128) * 128
        height = order - first_row
        width = order - first_col
        row_index = lax.broadcasted_iota(jnp.int32, (height, width), 0) + first_row
        col_index = lax.broadcasted_iota(jnp.int32, (height, width), 1) + first_col

        def step(column_index, carry):
            window = reduced_ref[first_row:, first_col:]
            pivot_line = reduced_ref[pl.ds(column_index, 1), :][:, first_col:]
            on_column = col_index == column_index
            pivot_column = jnp.sum(jnp.where(on_column, window, 0.0), axis=1, keepdims=True)
            pivot_value = jnp.sum(
                jnp.where(on_column[0:1], pivot_line, 0.0), axis=1, keepdims=True
            )
            factors = pivot_column / pivot_value
            below = row_index > column_index
            window = jnp.where(
                below & (col_index > column_index), window - factors * pivot_line, window
            )
            window = jnp.where(below & on_column, factors, window)
            reduced_ref[first_row:, first_col:] = window
            return carry

        lax.fori_loop(first_row, min(first_row + phase, order - 1), step, 0)


def factor(matrix):
    order = matrix.shape[0]
    reduced = pl.pallas_call(
        elimination_kernel,
        out_shape=jax.ShapeDtypeStruct(matrix.shape, matrix.dtype),
    )(matrix)
    lower = jnp.tril(reduced, -1) + jnp.eye(order, dtype=matrix.dtype)
    return (lower, jnp.triu(reduced))


def contract_first(left_side, right_side):
    return lax.dot_general(
        left_side, right_side, (((0,), (0,)), ((), ())), precision=full_precision
    )


def contract_second(left_side, right_side):
    return lax.dot_general(
        left_side, right_side, (((1,), (1,)), ((), ())), precision=full_precision
    )


def butterfly_sum(value, axis):
    levels = lax.axis_size(axis).bit_length() - 1
    for section in range(levels):
        value = value + from_partner(value, axis, section)
    return value


def body(panel_t, trailing, prev_lower_t, prev_upper, leaf_picks, merge_picks):
    slab_rows = panel_t.shape[0]
    rows_here = panel_t.shape[1]
    order = merge_picks.shape[1]
    row_devices = lax.axis_size("rows")
    own_row = lax.axis_index("rows")
    own_column = lax.axis_index("cols")
    leaf_group, leaf_slot = trace_pivots(merge_picks, row_devices)
    owner_mask = leaf_group == own_row
    local_rows = lookup(leaf_picks, jnp.zeros_like(leaf_slot), leaf_slot)
    own_trailing = jnp.take(trailing, local_rows, axis=0)
    own_columns = jnp.take(jnp.concatenate([panel_t, prev_lower_t], 0), local_rows, axis=1)
    own_pivots = jnp.concatenate([own_trailing, own_columns.T], 1)
    pivot_data = butterfly_sum(jnp.where(owner_mask[:, None], own_pivots, 0.0), "rows")
    pivot_trailing = pivot_data[:, : own_trailing.shape[1]]
    pivot_columns = lax.all_gather(
        pivot_data[:, own_trailing.shape[1] :].T, "cols", axis=0, tiled=False
    )
    block_t = pivot_columns[:, :slab_rows].reshape(order, order)
    prev_pivots = pivot_columns[:, slab_rows:].reshape(order, order)
    middle_pivots = pivot_trailing - contract_first(prev_pivots, prev_upper)
    middle = trailing - contract_first(
        lax.all_gather(prev_lower_t, "cols", axis=0, tiled=True), prev_upper
    )
    panel_full = lax.all_gather(panel_t, "cols", axis=0, tiled=True)
    lower_left, upper_left = factor(block_t.T)
    inverse = upper_inverse(upper_left)
    upper_right = product(unit_lower_inverse(lower_left), middle_pivots)
    lower_full = jnp.dot(inverse.T, panel_full, precision=full_precision)
    lower_tile = lax.dynamic_slice_in_dim(lower_full, own_column * slab_rows, slab_rows, 0)
    updated = middle - contract_first(lower_full, upper_right)
    gram_rows = contract_second(lower_tile, lower_full)
    gram = butterfly_sum(gram_rows, "rows") / (rows_here * row_devices)
    return (lower_tile, upper_left, upper_right, updated, gram)


def solution(mesh):
    return jax.shard_map(
        body,
        mesh=mesh,
        in_specs=(
            P("cols", "rows"),
            P("rows", "cols"),
            P("cols", "rows"),
            P(None, "cols"),
            P("rows", None),
            P(),
        ),
        out_specs=(P("cols", "rows"), P(), P(None, "cols"), P("rows", "cols"), P("cols", None)),
        check_vma=False,
    )
```

```python
import jax
import jax.numpy as jnp
from jax import lax
from jax.experimental import pallas as pl
from jax.experimental.pallas import tpu as pltpu
from jax.sharding import PartitionSpec as P

full_precision = lax.Precision.HIGHEST


def from_partner(shard, axis, apart):
    return lax.ppermute(shard, axis, [(i, i ^ 1 << apart) for i in range(lax.axis_size(axis))])


def lookup(table, group, slot):
    width = table.shape[1]
    slot_hit = slot[:, None] == lax.broadcasted_iota(jnp.int32, (slot.shape[0], width), 1)
    chosen = jnp.zeros((slot.shape[0], width), table.dtype)
    for index in range(table.shape[0]):
        chosen = jnp.where((group == index)[:, None], table[index][None, :], chosen)
    return jnp.sum(jnp.where(slot_hit, chosen, 0), axis=1)


def trace_pivots(merge_picks, row_devices):
    list_width = merge_picks.shape[1]
    leaf_group = jnp.zeros((list_width,), jnp.int32)
    leaf_slot = jnp.arange(list_width, dtype=jnp.int32)
    levels = row_devices.bit_length() - 1
    for section in reversed(range(levels)):
        offset_rows = row_devices - (row_devices >> section)
        groups = 1 << levels - 1 - section
        position = lookup(merge_picks[offset_rows : offset_rows + groups], leaf_group, leaf_slot)
        right_side = (position >= list_width).astype(jnp.int32)
        leaf_group = 2 * leaf_group + right_side
        leaf_slot = position - list_width * right_side
    return (leaf_group, leaf_slot)


def product(left_side, right_side):
    return jnp.dot(left_side, right_side, precision=full_precision)


def unit_lower_inverse(lower):
    order = lower.shape[0]
    identity = jnp.eye(order, dtype=jnp.float32)
    power = identity - lower
    result = identity + power
    covered = 1
    while covered < order - 1:
        power = product(power, power)
        result = product(result, identity + power)
        covered = 2 * covered + 1
    return result


def upper_inverse(upper):
    order = upper.shape[0]
    on_diagonal = lax.broadcasted_iota(jnp.int32, (order, order), 0) == lax.broadcasted_iota(
        jnp.int32, (order, order), 1
    )
    diagonal = jnp.sum(jnp.where(on_diagonal, upper, 0.0), axis=0)
    scaled = upper / diagonal[:, None]
    unit_inverse = unit_lower_inverse(scaled.T).T
    return unit_inverse / diagonal[None, :]


def elimination_kernel(matrix_ref, reduced_ref):
    order = matrix_ref.shape[0]
    reduced_ref[...] = matrix_ref[...]
    phase = 32
    for first_row in range(0, order, phase):
        first_col = (first_row // 128) * 128
        height = order - first_row
        width = order - first_col
        lanes = min(128, width)
        row_index = lax.broadcasted_iota(jnp.int32, (height, 1), 0) + first_row
        col_index = lax.broadcasted_iota(jnp.int32, (1, width), 1) + first_col
        block_index = lax.broadcasted_iota(jnp.int32, (height, lanes), 1) + first_col

        def step(pair, carry):
            first = first_row + 2 * pair
            second = first + 1
            window = reduced_ref[first_row:, first_col:]
            first_line = reduced_ref[pl.ds(first, 1), :][:, first_col:]
            second_line = reduced_ref[pl.ds(second, 1), :][:, first_col:]
            lead = window[:, :lanes]
            on_first = block_index == first
            on_second = block_index == second
            first_column = jnp.sum(jnp.where(on_first, lead, 0.0), axis=1, keepdims=True)
            second_column = jnp.sum(jnp.where(on_second, lead, 0.0), axis=1, keepdims=True)
            first_pivot = jnp.sum(
                jnp.where(col_index == first, first_line, 0.0), axis=1, keepdims=True
            )
            coupling = jnp.sum(
                jnp.where(col_index == second, first_line, 0.0), axis=1, keepdims=True
            )
            second_lead = jnp.sum(
                jnp.where(col_index == first, second_line, 0.0), axis=1, keepdims=True
            )
            below_first = row_index > first
            below_second = row_index > second
            first_factors = jnp.where(below_first, first_column / first_pivot, 0.0)
            first_line = jnp.where(col_index > first, first_line, 0.0)
            second_line = second_line - second_lead / first_pivot * first_line
            second_column = second_column - first_factors * coupling
            second_pivot = jnp.sum(
                jnp.where(col_index == second, second_line, 0.0), axis=1, keepdims=True
            )
            second_factors = jnp.where(below_second, second_column / second_pivot, 0.0)
            second_line = jnp.where(col_index > second, second_line, 0.0)
            window = window - first_factors * first_line - second_factors * second_line
            first_kept = jnp.where(below_first, first_factors, first_column)
            second_kept = jnp.where(below_second, second_factors, second_column)
            reduced_ref[first_row:, first_col:] = window
            reduced_ref[first_row:, first_col : first_col + lanes] = jnp.where(
                on_first, first_kept, jnp.where(on_second, second_kept, window[:, :lanes])
            )
            return carry

        lax.fori_loop(0, min(phase, order - first_row) // 2, step, 0)


def factor(matrix):
    order = matrix.shape[0]
    reduced = pl.pallas_call(
        elimination_kernel,
        out_shape=jax.ShapeDtypeStruct(matrix.shape, matrix.dtype),
    )(matrix)
    lower = jnp.tril(reduced, -1) + jnp.eye(order, dtype=matrix.dtype)
    return (lower, jnp.triu(reduced))


def contract_first(left_side, right_side):
    return lax.dot_general(
        left_side, right_side, (((0,), (0,)), ((), ())), precision=full_precision
    )


def contract_second(left_side, right_side):
    return lax.dot_general(
        left_side, right_side, (((1,), (1,)), ((), ())), precision=full_precision
    )


def butterfly_sum(value, axis):
    levels = lax.axis_size(axis).bit_length() - 1
    for section in range(levels):
        value = value + from_partner(value, axis, section)
    return value


def body(panel_t, trailing, prev_lower_t, prev_upper, leaf_picks, merge_picks):
    slab_rows = panel_t.shape[0]
    rows_here = panel_t.shape[1]
    order = merge_picks.shape[1]
    row_devices = lax.axis_size("rows")
    own_row = lax.axis_index("rows")
    own_column = lax.axis_index("cols")
    leaf_group, leaf_slot = trace_pivots(merge_picks, row_devices)
    owner_mask = leaf_group == own_row
    local_rows = lookup(leaf_picks, jnp.zeros_like(leaf_slot), leaf_slot)
    own_trailing = jnp.take(trailing, local_rows, axis=0)
    own_columns = jnp.take(jnp.concatenate([panel_t, prev_lower_t], 0), local_rows, axis=1)
    own_pivots = jnp.concatenate([own_trailing, own_columns.T], 1)
    pivot_data = butterfly_sum(jnp.where(owner_mask[:, None], own_pivots, 0.0), "rows")
    pivot_trailing = pivot_data[:, : own_trailing.shape[1]]
    pivot_columns = lax.all_gather(
        pivot_data[:, own_trailing.shape[1] :].T, "cols", axis=0, tiled=False
    )
    block_t = pivot_columns[:, :slab_rows].reshape(order, order)
    prev_pivots = pivot_columns[:, slab_rows:].reshape(order, order)
    middle_pivots = pivot_trailing - contract_first(prev_pivots, prev_upper)
    middle = trailing - contract_first(
        lax.all_gather(prev_lower_t, "cols", axis=0, tiled=True), prev_upper
    )
    panel_full = lax.all_gather(panel_t, "cols", axis=0, tiled=True)
    lower_left, upper_left = factor(block_t.T)
    inverse = upper_inverse(upper_left)
    upper_right = product(unit_lower_inverse(lower_left), middle_pivots)
    lower_full = jnp.dot(inverse.T, panel_full, precision=full_precision)
    lower_tile = lax.dynamic_slice_in_dim(lower_full, own_column * slab_rows, slab_rows, 0)
    updated = middle - contract_first(lower_full, upper_right)
    gram_rows = contract_second(lower_tile, lower_full)
    gram = butterfly_sum(gram_rows, "rows") / (rows_here * row_devices)
    return (lower_tile, upper_left, upper_right, updated, gram)


def solution(mesh):
    return jax.shard_map(
        body,
        mesh=mesh,
        in_specs=(
            P("cols", "rows"),
            P("rows", "cols"),
            P("cols", "rows"),
            P(None, "cols"),
            P("rows", None),
            P(),
        ),
        out_specs=(P("cols", "rows"), P(), P(None, "cols"), P("rows", "cols"), P("cols", None)),
        check_vma=False,
    )
```

```python
import jax
import jax.numpy as jnp
from jax import lax
from jax.experimental import pallas as pl
from jax.experimental.pallas import tpu as pltpu
from jax.sharding import PartitionSpec as P

full_precision = lax.Precision.HIGHEST


def from_partner(shard, axis, apart):
    return lax.ppermute(shard, axis, [(i, i ^ 1 << apart) for i in range(lax.axis_size(axis))])


def lookup(table, group, slot):
    width = table.shape[1]
    slot_hit = slot[:, None] == lax.broadcasted_iota(jnp.int32, (slot.shape[0], width), 1)
    chosen = jnp.zeros((slot.shape[0], width), table.dtype)
    for index in range(table.shape[0]):
        chosen = jnp.where((group == index)[:, None], table[index][None, :], chosen)
    return jnp.sum(jnp.where(slot_hit, chosen, 0), axis=1)


def trace_pivots(merge_picks, row_devices):
    list_width = merge_picks.shape[1]
    leaf_group = jnp.zeros((list_width,), jnp.int32)
    leaf_slot = jnp.arange(list_width, dtype=jnp.int32)
    levels = row_devices.bit_length() - 1
    for section in reversed(range(levels)):
        offset_rows = row_devices - (row_devices >> section)
        groups = 1 << levels - 1 - section
        position = lookup(merge_picks[offset_rows : offset_rows + groups], leaf_group, leaf_slot)
        right_side = (position >= list_width).astype(jnp.int32)
        leaf_group = 2 * leaf_group + right_side
        leaf_slot = position - list_width * right_side
    return (leaf_group, leaf_slot)


def product(left_side, right_side):
    return jnp.dot(left_side, right_side, precision=full_precision)


def unit_lower_inverse(lower):
    order = lower.shape[0]
    identity = jnp.eye(order, dtype=jnp.float32)
    power = identity - lower
    result = identity + power
    covered = 1
    while covered < order - 1:
        power = product(power, power)
        result = product(result, identity + power)
        covered = 2 * covered + 1
    return result


def upper_inverse(upper):
    order = upper.shape[0]
    on_diagonal = lax.broadcasted_iota(jnp.int32, (order, order), 0) == lax.broadcasted_iota(
        jnp.int32, (order, order), 1
    )
    diagonal = jnp.sum(jnp.where(on_diagonal, upper, 0.0), axis=0)
    scaled = upper / diagonal[:, None]
    unit_inverse = unit_lower_inverse(scaled.T).T
    return unit_inverse / diagonal[None, :]


def elimination_kernel(matrix_ref, reduced_ref):
    order = matrix_ref.shape[0]
    reduced_ref[...] = matrix_ref[...]
    phase = 32
    for first_row in range(0, order, phase):
        first_col = (first_row // 128) * 128
        height = order - first_row
        width = order - first_col
        lanes = min(128, width)
        row_index = lax.broadcasted_iota(jnp.int32, (height, 1), 0) + first_row
        col_index = lax.broadcasted_iota(jnp.int32, (1, width), 1) + first_col
        block_index = lax.broadcasted_iota(jnp.int32, (height, lanes), 1) + first_col

        def step(pair, carry):
            first = first_row + 2 * pair
            second = first + 1
            window = reduced_ref[first_row:, first_col:]
            first_line = reduced_ref[pl.ds(first, 1), :][:, first_col:]
            second_line = reduced_ref[pl.ds(second, 1), :][:, first_col:]
            lead = window[:, :lanes]
            on_first = block_index == first
            on_second = block_index == second
            first_column = jnp.sum(jnp.where(on_first, lead, 0.0), axis=1, keepdims=True)
            second_column = jnp.sum(jnp.where(on_second, lead, 0.0), axis=1, keepdims=True)
            first_pivot = jnp.sum(
                jnp.where(col_index == first, first_line, 0.0), axis=1, keepdims=True
            )
            coupling = jnp.sum(
                jnp.where(col_index == second, first_line, 0.0), axis=1, keepdims=True
            )
            second_lead = jnp.sum(
                jnp.where(col_index == first, second_line, 0.0), axis=1, keepdims=True
            )
            below_first = row_index > first
            below_second = row_index > second
            first_factors = jnp.where(below_first, first_column / first_pivot, 0.0)
            first_line = jnp.where(col_index > first, first_line, 0.0)
            second_line = second_line - second_lead / first_pivot * first_line
            second_column = second_column - first_factors * coupling
            second_pivot = jnp.sum(
                jnp.where(col_index == second, second_line, 0.0), axis=1, keepdims=True
            )
            second_factors = jnp.where(below_second, second_column / second_pivot, 0.0)
            second_line = jnp.where(col_index > second, second_line, 0.0)
            window = window - first_factors * first_line - second_factors * second_line
            first_kept = jnp.where(below_first, first_factors, first_column)
            second_kept = jnp.where(below_second, second_factors, second_column)
            reduced_ref[first_row:, first_col:] = window
            reduced_ref[first_row:, first_col : first_col + lanes] = jnp.where(
                on_first, first_kept, jnp.where(on_second, second_kept, window[:, :lanes])
            )
            return carry

        lax.fori_loop(0, min(phase, order - first_row) // 2, step, 0)


def factor(matrix):
    order = matrix.shape[0]
    reduced = pl.pallas_call(
        elimination_kernel,
        out_shape=jax.ShapeDtypeStruct(matrix.shape, matrix.dtype),
    )(matrix)
    lower = jnp.tril(reduced, -1) + jnp.eye(order, dtype=matrix.dtype)
    return (lower, jnp.triu(reduced))


def contract_first(left_side, right_side):
    return lax.dot_general(
        left_side, right_side, (((0,), (0,)), ((), ())), precision=full_precision
    )


def contract_second(left_side, right_side):
    return lax.dot_general(
        left_side, right_side, (((1,), (1,)), ((), ())), precision=full_precision
    )


def butterfly_sum(value, axis):
    levels = lax.axis_size(axis).bit_length() - 1
    for section in range(levels):
        value = value + from_partner(value, axis, section)
    return value


def body(panel_t, trailing, prev_lower_t, prev_upper, leaf_picks, merge_picks):
    slab_rows = panel_t.shape[0]
    rows_here = panel_t.shape[1]
    order = merge_picks.shape[1]
    row_devices = lax.axis_size("rows")
    own_row = lax.axis_index("rows")
    own_column = lax.axis_index("cols")
    leaf_group, leaf_slot = trace_pivots(merge_picks, row_devices)
    owner_mask = leaf_group == own_row
    local_rows = lookup(leaf_picks, jnp.zeros_like(leaf_slot), leaf_slot)
    own_trailing = jnp.take(trailing, local_rows, axis=0)
    own_columns = jnp.take(jnp.concatenate([panel_t, prev_lower_t], 0), local_rows, axis=1)
    own_pivots = jnp.concatenate([own_trailing, own_columns.T], 1)
    pivot_data = butterfly_sum(jnp.where(owner_mask[:, None], own_pivots, 0.0), "rows")
    pivot_trailing = pivot_data[:, : own_trailing.shape[1]]
    pivot_columns = lax.all_gather(
        pivot_data[:, own_trailing.shape[1] :].T, "cols", axis=0, tiled=False
    )
    block_t = pivot_columns[:, :slab_rows].reshape(order, order)
    prev_pivots = pivot_columns[:, slab_rows:].reshape(order, order)
    middle_pivots = pivot_trailing - contract_first(prev_pivots, prev_upper)
    prev_full = lax.all_gather(prev_lower_t, "cols", axis=0, tiled=True)
    panel_full = lax.all_gather(panel_t, "cols", axis=0, tiled=True)
    gram_part, block_t = lax.optimization_barrier((contract_second(panel_full, panel_full), block_t))
    panel_gram = butterfly_sum(gram_part, "rows")
    lower_left, upper_left = factor(block_t.T)
    inverse = upper_inverse(upper_left)
    upper_right = product(unit_lower_inverse(lower_left), middle_pivots)
    lower_full = jnp.dot(inverse.T, panel_full, precision=full_precision)
    prev_full, lower_full = lax.optimization_barrier((prev_full, lower_full))
    middle = trailing - contract_first(prev_full, prev_upper)
    lower_tile = lax.dynamic_slice_in_dim(lower_full, own_column * slab_rows, slab_rows, 0)
    updated = middle - contract_first(lower_full, upper_right)
    inverse_tile = lax.dynamic_slice_in_dim(inverse, own_column * slab_rows, slab_rows, 1)
    gram_rows = contract_first(inverse_tile, product(panel_gram, inverse))
    gram = gram_rows / (rows_here * row_devices)
    return (lower_tile, upper_left, upper_right, updated, gram)


def solution(mesh):
    return jax.shard_map(
        body,
        mesh=mesh,
        in_specs=(
            P("cols", "rows"),
            P("rows", "cols"),
            P("cols", "rows"),
            P(None, "cols"),
            P("rows", None),
            P(),
        ),
        out_specs=(P("cols", "rows"), P(), P(None, "cols"), P("rows", "cols"), P("cols", None)),
        check_vma=False,
    )
```

```python
import jax
import jax.numpy as jnp
from jax import lax
from jax.experimental import pallas as pl
from jax.experimental.pallas import tpu as pltpu
from jax.sharding import PartitionSpec as P

full_precision = lax.Precision.HIGHEST


def from_partner(shard, axis, apart):
    return lax.ppermute(shard, axis, [(i, i ^ 1 << apart) for i in range(lax.axis_size(axis))])


def lookup(table, group, slot):
    width = table.shape[1]
    slot_hit = slot[:, None] == lax.broadcasted_iota(jnp.int32, (slot.shape[0], width), 1)
    chosen = jnp.zeros((slot.shape[0], width), table.dtype)
    for index in range(table.shape[0]):
        chosen = jnp.where((group == index)[:, None], table[index][None, :], chosen)
    return jnp.sum(jnp.where(slot_hit, chosen, 0), axis=1)


def trace_pivots(merge_picks, row_devices):
    list_width = merge_picks.shape[1]
    leaf_group = jnp.zeros((list_width,), jnp.int32)
    leaf_slot = jnp.arange(list_width, dtype=jnp.int32)
    levels = row_devices.bit_length() - 1
    for section in reversed(range(levels)):
        offset_rows = row_devices - (row_devices >> section)
        groups = 1 << levels - 1 - section
        position = lookup(merge_picks[offset_rows : offset_rows + groups], leaf_group, leaf_slot)
        right_side = (position >= list_width).astype(jnp.int32)
        leaf_group = 2 * leaf_group + right_side
        leaf_slot = position - list_width * right_side
    return (leaf_group, leaf_slot)


def product(left_side, right_side):
    return jnp.dot(left_side, right_side, precision=full_precision)


def unit_lower_inverse(lower):
    order = lower.shape[0]
    identity = jnp.eye(order, dtype=jnp.float32)
    power = identity - lower
    result = identity + power
    covered = 1
    while covered < order - 1:
        power = product(power, power)
        result = product(result, identity + power)
        covered = 2 * covered + 1
    return result


def upper_inverse(upper):
    order = upper.shape[0]
    on_diagonal = lax.broadcasted_iota(jnp.int32, (order, order), 0) == lax.broadcasted_iota(
        jnp.int32, (order, order), 1
    )
    diagonal = jnp.sum(jnp.where(on_diagonal, upper, 0.0), axis=0)
    scaled = upper / diagonal[:, None]
    unit_inverse = unit_lower_inverse(scaled.T).T
    return unit_inverse / diagonal[None, :]


def elimination_kernel(matrix_ref, reduced_ref):
    order = matrix_ref.shape[0]
    reduced_ref[...] = matrix_ref[...]
    phase = 32
    for first_row in range(0, order, phase):
        first_col = (first_row // 128) * 128
        height = order - first_row
        width = order - first_col
        lanes = min(128, width)
        row_index = lax.broadcasted_iota(jnp.int32, (height, 1), 0) + first_row
        col_index = lax.broadcasted_iota(jnp.int32, (1, width), 1) + first_col
        block_index = lax.broadcasted_iota(jnp.int32, (height, lanes), 1) + first_col

        def step(pair, carry):
            first = first_row + 2 * pair
            second = first + 1
            window = reduced_ref[first_row:, first_col:]
            first_line = reduced_ref[pl.ds(first, 1), :][:, first_col:]
            second_line = reduced_ref[pl.ds(second, 1), :][:, first_col:]
            lead = window[:, :lanes]
            on_first = block_index == first
            on_second = block_index == second
            first_column = jnp.sum(jnp.where(on_first, lead, 0.0), axis=1, keepdims=True)
            second_column = jnp.sum(jnp.where(on_second, lead, 0.0), axis=1, keepdims=True)
            first_pivot = jnp.sum(
                jnp.where(col_index == first, first_line, 0.0), axis=1, keepdims=True
            )
            coupling = jnp.sum(
                jnp.where(col_index == second, first_line, 0.0), axis=1, keepdims=True
            )
            second_lead = jnp.sum(
                jnp.where(col_index == first, second_line, 0.0), axis=1, keepdims=True
            )
            below_first = row_index > first
            below_second = row_index > second
            first_factors = jnp.where(below_first, first_column / first_pivot, 0.0)
            first_line = jnp.where(col_index > first, first_line, 0.0)
            second_line = second_line - second_lead / first_pivot * first_line
            second_column = second_column - first_factors * coupling
            second_pivot = jnp.sum(
                jnp.where(col_index == second, second_line, 0.0), axis=1, keepdims=True
            )
            second_factors = jnp.where(below_second, second_column / second_pivot, 0.0)
            second_line = jnp.where(col_index > second, second_line, 0.0)
            window = window - first_factors * first_line - second_factors * second_line
            first_kept = jnp.where(below_first, first_factors, first_column)
            second_kept = jnp.where(below_second, second_factors, second_column)
            reduced_ref[first_row:, first_col:] = window
            reduced_ref[first_row:, first_col : first_col + lanes] = jnp.where(
                on_first, first_kept, jnp.where(on_second, second_kept, window[:, :lanes])
            )
            return carry

        lax.fori_loop(0, min(phase, order - first_row) // 2, step, 0)


def factor(matrix):
    order = matrix.shape[0]
    reduced = pl.pallas_call(
        elimination_kernel,
        out_shape=jax.ShapeDtypeStruct(matrix.shape, matrix.dtype),
    )(matrix)
    lower = jnp.tril(reduced, -1) + jnp.eye(order, dtype=matrix.dtype)
    return (lower, jnp.triu(reduced))


def contract_first(left_side, right_side):
    return lax.dot_general(
        left_side, right_side, (((0,), (0,)), ((), ())), precision=full_precision
    )


def contract_second(left_side, right_side):
    return lax.dot_general(
        left_side, right_side, (((1,), (1,)), ((), ())), precision=full_precision
    )


def butterfly_sum(value, axis):
    levels = lax.axis_size(axis).bit_length() - 1
    for section in range(levels):
        value = value + from_partner(value, axis, section)
    return value


def body(panel_t, trailing, prev_lower_t, prev_upper, leaf_picks, merge_picks):
    slab_rows = panel_t.shape[0]
    rows_here = panel_t.shape[1]
    order = merge_picks.shape[1]
    row_devices = lax.axis_size("rows")
    own_row = lax.axis_index("rows")
    own_column = lax.axis_index("cols")
    leaf_group, leaf_slot = trace_pivots(merge_picks, row_devices)
    owner_mask = leaf_group == own_row
    local_rows = lookup(leaf_picks, jnp.zeros_like(leaf_slot), leaf_slot)
    own_trailing = jnp.take(trailing, local_rows, axis=0)
    own_columns = jnp.take(jnp.concatenate([panel_t, prev_lower_t], 0), local_rows, axis=1)
    own_pivots = jnp.concatenate([own_trailing, own_columns.T], 1)
    pivot_data = butterfly_sum(jnp.where(owner_mask[:, None], own_pivots, 0.0), "rows")
    pivot_trailing = pivot_data[:, : own_trailing.shape[1]]
    pivot_columns = lax.all_gather(
        pivot_data[:, own_trailing.shape[1] :].T, "cols", axis=0, tiled=False
    )
    block_t = pivot_columns[:, :slab_rows].reshape(order, order)
    prev_pivots = pivot_columns[:, slab_rows:].reshape(order, order)
    middle_pivots = pivot_trailing - contract_first(prev_pivots, prev_upper)
    middle = trailing - contract_first(
        lax.all_gather(prev_lower_t, "cols", axis=0, tiled=True), prev_upper
    )
    panel_full = lax.all_gather(panel_t, "cols", axis=0, tiled=True)
    lower_left, upper_left = factor(block_t.T)
    inverse = upper_inverse(upper_left)
    lower_full = jnp.dot(inverse.T, panel_full, precision=full_precision)
    lower_tile = lax.dynamic_slice_in_dim(lower_full, own_column * slab_rows, slab_rows, 0)
    gram_rows = contract_second(lower_tile, lower_full)
    lower_left, gram_rows = lax.optimization_barrier((lower_left, gram_rows))
    gram = butterfly_sum(gram_rows, "rows") / (rows_here * row_devices)
    upper_right = product(unit_lower_inverse(lower_left), middle_pivots)
    updated = middle - contract_first(lower_full, upper_right)
    return (lower_tile, upper_left, upper_right, updated, gram)


def solution(mesh):
    return jax.shard_map(
        body,
        mesh=mesh,
        in_specs=(
            P("cols", "rows"),
            P("rows", "cols"),
            P("cols", "rows"),
            P(None, "cols"),
            P("rows", None),
            P(),
        ),
        out_specs=(P("cols", "rows"), P(), P(None, "cols"), P("rows", "cols"), P("cols", None)),
        check_vma=False,
    )
```

```python
import jax
import jax.numpy as jnp
from jax import lax
from jax.experimental import pallas as pl
from jax.experimental.pallas import tpu as pltpu
from jax.sharding import PartitionSpec as P

full_precision = lax.Precision.HIGHEST


def from_partner(shard, axis, apart):
    return lax.ppermute(shard, axis, [(i, i ^ 1 << apart) for i in range(lax.axis_size(axis))])


def lookup(table, group, slot):
    width = table.shape[1]
    slot_hit = slot[:, None] == lax.broadcasted_iota(jnp.int32, (slot.shape[0], width), 1)
    chosen = jnp.zeros((slot.shape[0], width), table.dtype)
    for index in range(table.shape[0]):
        chosen = jnp.where((group == index)[:, None], table[index][None, :], chosen)
    return jnp.sum(jnp.where(slot_hit, chosen, 0), axis=1)


def trace_pivots(merge_picks, row_devices):
    list_width = merge_picks.shape[1]
    leaf_group = jnp.zeros((list_width,), jnp.int32)
    leaf_slot = jnp.arange(list_width, dtype=jnp.int32)
    levels = row_devices.bit_length() - 1
    for section in reversed(range(levels)):
        offset_rows = row_devices - (row_devices >> section)
        groups = 1 << levels - 1 - section
        position = lookup(merge_picks[offset_rows : offset_rows + groups], leaf_group, leaf_slot)
        right_side = (position >= list_width).astype(jnp.int32)
        leaf_group = 2 * leaf_group + right_side
        leaf_slot = position - list_width * right_side
    return (leaf_group, leaf_slot)


def product(left_side, right_side):
    return jnp.dot(left_side, right_side, precision=full_precision)


def unit_lower_inverse(lower):
    order = lower.shape[0]
    identity = jnp.eye(order, dtype=jnp.float32)
    power = identity - lower
    result = identity + power
    covered = 1
    while covered < order - 1:
        power = product(power, power)
        result = product(result, identity + power)
        covered = 2 * covered + 1
    return result


def upper_inverse(upper):
    order = upper.shape[0]
    on_diagonal = lax.broadcasted_iota(jnp.int32, (order, order), 0) == lax.broadcasted_iota(
        jnp.int32, (order, order), 1
    )
    diagonal = jnp.sum(jnp.where(on_diagonal, upper, 0.0), axis=0)
    scaled = upper / diagonal[:, None]
    unit_inverse = unit_lower_inverse(scaled.T).T
    return unit_inverse / diagonal[None, :]


def elimination_kernel(matrix_ref, reduced_ref):
    order = matrix_ref.shape[0]
    reduced_ref[...] = matrix_ref[...]
    phase = 32
    for first_row in range(0, order, phase):
        first_col = (first_row // 128) * 128
        height = order - first_row
        width = order - first_col
        lanes = min(128, width)
        row_index = lax.broadcasted_iota(jnp.int32, (height, 1), 0) + first_row
        col_index = lax.broadcasted_iota(jnp.int32, (1, width), 1) + first_col
        block_index = lax.broadcasted_iota(jnp.int32, (height, lanes), 1) + first_col

        def step(pair, carry):
            first = first_row + 2 * pair
            second = first + 1
            window = reduced_ref[first_row:, first_col:]
            first_line = reduced_ref[pl.ds(first, 1), :][:, first_col:]
            second_line = reduced_ref[pl.ds(second, 1), :][:, first_col:]
            lead = window[:, :lanes]
            on_first = block_index == first
            on_second = block_index == second
            first_column = jnp.sum(jnp.where(on_first, lead, 0.0), axis=1, keepdims=True)
            second_column = jnp.sum(jnp.where(on_second, lead, 0.0), axis=1, keepdims=True)
            first_pivot = jnp.sum(
                jnp.where(col_index == first, first_line, 0.0), axis=1, keepdims=True
            )
            coupling = jnp.sum(
                jnp.where(col_index == second, first_line, 0.0), axis=1, keepdims=True
            )
            second_lead = jnp.sum(
                jnp.where(col_index == first, second_line, 0.0), axis=1, keepdims=True
            )
            below_first = row_index > first
            below_second = row_index > second
            first_factors = jnp.where(below_first, first_column / first_pivot, 0.0)
            first_line = jnp.where(col_index > first, first_line, 0.0)
            second_line = second_line - second_lead / first_pivot * first_line
            second_column = second_column - first_factors * coupling
            second_pivot = jnp.sum(
                jnp.where(col_index == second, second_line, 0.0), axis=1, keepdims=True
            )
            second_factors = jnp.where(below_second, second_column / second_pivot, 0.0)
            second_line = jnp.where(col_index > second, second_line, 0.0)
            window = window - first_factors * first_line - second_factors * second_line
            first_kept = jnp.where(below_first, first_factors, first_column)
            second_kept = jnp.where(below_second, second_factors, second_column)
            reduced_ref[first_row:, first_col:] = window
            reduced_ref[first_row:, first_col : first_col + lanes] = jnp.where(
                on_first, first_kept, jnp.where(on_second, second_kept, window[:, :lanes])
            )
            return carry

        lax.fori_loop(0, min(phase, order - first_row) // 2, step, 0)


def factor(matrix):
    order = matrix.shape[0]
    reduced = pl.pallas_call(
        elimination_kernel,
        out_shape=jax.ShapeDtypeStruct(matrix.shape, matrix.dtype),
    )(matrix)
    lower = jnp.tril(reduced, -1) + jnp.eye(order, dtype=matrix.dtype)
    return (lower, jnp.triu(reduced))


def contract_first(left_side, right_side):
    return lax.dot_general(
        left_side, right_side, (((0,), (0,)), ((), ())), precision=full_precision
    )


def contract_second(left_side, right_side):
    return lax.dot_general(
        left_side, right_side, (((1,), (1,)), ((), ())), precision=full_precision
    )


def butterfly_sum(value, axis):
    levels = lax.axis_size(axis).bit_length() - 1
    for section in range(levels):
        value = value + from_partner(value, axis, section)
    return value


def body(panel_t, trailing, prev_lower_t, prev_upper, leaf_picks, merge_picks):
    slab_rows = panel_t.shape[0]
    rows_here = panel_t.shape[1]
    order = merge_picks.shape[1]
    row_devices = lax.axis_size("rows")
    own_row = lax.axis_index("rows")
    own_column = lax.axis_index("cols")
    leaf_group, leaf_slot = trace_pivots(merge_picks, row_devices)
    owner_mask = leaf_group == own_row
    local_rows = lookup(leaf_picks, jnp.zeros_like(leaf_slot), leaf_slot)
    own_columns = jnp.take(jnp.concatenate([panel_t, prev_lower_t], 0), local_rows, axis=1)
    pivot_part = butterfly_sum(jnp.where(owner_mask[None, :], own_columns, 0.0), "rows")
    pivot_columns = lax.all_gather(pivot_part, "cols", axis=0, tiled=False)
    own_trailing = jnp.take(trailing, local_rows, axis=0)
    own_trailing = jnp.where(owner_mask[:, None], own_trailing, 0.0)
    own_trailing, pivot_columns = lax.optimization_barrier((own_trailing, pivot_columns))
    pivot_trailing = butterfly_sum(own_trailing, "rows")
    block_t = pivot_columns[:, :slab_rows].reshape(order, order)
    prev_pivots = pivot_columns[:, slab_rows:].reshape(order, order)
    middle_pivots = pivot_trailing - contract_first(prev_pivots, prev_upper)
    middle = trailing - contract_first(
        lax.all_gather(prev_lower_t, "cols", axis=0, tiled=True), prev_upper
    )
    panel_full = lax.all_gather(panel_t, "cols", axis=0, tiled=True)
    lower_left, upper_left = factor(block_t.T)
    inverse = upper_inverse(upper_left)
    upper_right = product(unit_lower_inverse(lower_left), middle_pivots)
    lower_full = jnp.dot(inverse.T, panel_full, precision=full_precision)
    lower_tile = lax.dynamic_slice_in_dim(lower_full, own_column * slab_rows, slab_rows, 0)
    updated = middle - contract_first(lower_full, upper_right)
    gram_rows = contract_second(lower_tile, lower_full)
    gram = butterfly_sum(gram_rows, "rows") / (rows_here * row_devices)
    return (lower_tile, upper_left, upper_right, updated, gram)


def solution(mesh):
    return jax.shard_map(
        body,
        mesh=mesh,
        in_specs=(
            P("cols", "rows"),
            P("rows", "cols"),
            P("cols", "rows"),
            P(None, "cols"),
            P("rows", None),
            P(),
        ),
        out_specs=(P("cols", "rows"), P(), P(None, "cols"), P("rows", "cols"), P("cols", None)),
        check_vma=False,
    )
```

```python
import jax
import jax.numpy as jnp
from jax import lax
from jax.experimental import pallas as pl
from jax.experimental.pallas import tpu as pltpu
from jax.sharding import PartitionSpec as P

full_precision = lax.Precision.HIGHEST


def from_partner(shard, axis, apart):
    return lax.ppermute(shard, axis, [(i, i ^ 1 << apart) for i in range(lax.axis_size(axis))])


def lookup(table, group, slot):
    width = table.shape[1]
    slot_hit = slot[:, None] == lax.broadcasted_iota(jnp.int32, (slot.shape[0], width), 1)
    chosen = jnp.zeros((slot.shape[0], width), table.dtype)
    for index in range(table.shape[0]):
        chosen = jnp.where((group == index)[:, None], table[index][None, :], chosen)
    return jnp.sum(jnp.where(slot_hit, chosen, 0), axis=1)


def trace_pivots(merge_picks, row_devices):
    list_width = merge_picks.shape[1]
    leaf_group = jnp.zeros((list_width,), jnp.int32)
    leaf_slot = jnp.arange(list_width, dtype=jnp.int32)
    levels = row_devices.bit_length() - 1
    for section in reversed(range(levels)):
        offset_rows = row_devices - (row_devices >> section)
        groups = 1 << levels - 1 - section
        position = lookup(merge_picks[offset_rows : offset_rows + groups], leaf_group, leaf_slot)
        right_side = (position >= list_width).astype(jnp.int32)
        leaf_group = 2 * leaf_group + right_side
        leaf_slot = position - list_width * right_side
    return (leaf_group, leaf_slot)


def product(left_side, right_side):
    return jnp.dot(left_side, right_side, precision=full_precision)


def unit_lower_inverse(lower):
    order = lower.shape[0]
    identity = jnp.eye(order, dtype=jnp.float32)
    power = identity - lower
    result = identity + power
    covered = 1
    while covered < order - 1:
        power = product(power, power)
        result = product(result, identity + power)
        covered = 2 * covered + 1
    return result


def upper_inverse(upper):
    order = upper.shape[0]
    on_diagonal = lax.broadcasted_iota(jnp.int32, (order, order), 0) == lax.broadcasted_iota(
        jnp.int32, (order, order), 1
    )
    diagonal = jnp.sum(jnp.where(on_diagonal, upper, 0.0), axis=0)
    scaled = upper / diagonal[:, None]
    unit_inverse = unit_lower_inverse(scaled.T).T
    return unit_inverse / diagonal[None, :]


def elimination_kernel(matrix_ref, reduced_ref):
    order = matrix_ref.shape[0]
    reduced_ref[...] = matrix_ref[...]
    phase = 32
    for first_row in range(0, order, phase):
        first_col = (first_row // 128) * 128
        height = order - first_row
        width = order - first_col
        lanes = min(128, width)
        row_index = lax.broadcasted_iota(jnp.int32, (height, 1), 0) + first_row
        col_index = lax.broadcasted_iota(jnp.int32, (1, width), 1) + first_col
        block_index = lax.broadcasted_iota(jnp.int32, (height, lanes), 1) + first_col

        def step(pair, carry):
            first = first_row + 2 * pair
            second = first + 1
            window = reduced_ref[first_row:, first_col:]
            first_line = reduced_ref[pl.ds(first, 1), :][:, first_col:]
            second_line = reduced_ref[pl.ds(second, 1), :][:, first_col:]
            lead = window[:, :lanes]
            on_first = block_index == first
            on_second = block_index == second
            first_column = jnp.sum(jnp.where(on_first, lead, 0.0), axis=1, keepdims=True)
            second_column = jnp.sum(jnp.where(on_second, lead, 0.0), axis=1, keepdims=True)
            first_pivot = jnp.sum(
                jnp.where(col_index == first, first_line, 0.0), axis=1, keepdims=True
            )
            coupling = jnp.sum(
                jnp.where(col_index == second, first_line, 0.0), axis=1, keepdims=True
            )
            second_lead = jnp.sum(
                jnp.where(col_index == first, second_line, 0.0), axis=1, keepdims=True
            )
            below_first = row_index > first
            below_second = row_index > second
            first_factors = jnp.where(below_first, first_column / first_pivot, 0.0)
            first_line = jnp.where(col_index > first, first_line, 0.0)
            second_line = second_line - second_lead / first_pivot * first_line
            second_column = second_column - first_factors * coupling
            second_pivot = jnp.sum(
                jnp.where(col_index == second, second_line, 0.0), axis=1, keepdims=True
            )
            second_factors = jnp.where(below_second, second_column / second_pivot, 0.0)
            second_line = jnp.where(col_index > second, second_line, 0.0)
            window = window - first_factors * first_line - second_factors * second_line
            first_kept = jnp.where(below_first, first_factors, first_column)
            second_kept = jnp.where(below_second, second_factors, second_column)
            reduced_ref[first_row:, first_col:] = window
            reduced_ref[first_row:, first_col : first_col + lanes] = jnp.where(
                on_first, first_kept, jnp.where(on_second, second_kept, window[:, :lanes])
            )
            return carry

        lax.fori_loop(0, min(phase, order - first_row) // 2, step, 0)


def factor(matrix):
    order = matrix.shape[0]
    reduced = pl.pallas_call(
        elimination_kernel,
        out_shape=jax.ShapeDtypeStruct(matrix.shape, matrix.dtype),
    )(matrix)
    lower = jnp.tril(reduced, -1) + jnp.eye(order, dtype=matrix.dtype)
    return (lower, jnp.triu(reduced))


def contract_first(left_side, right_side):
    return lax.dot_general(
        left_side, right_side, (((0,), (0,)), ((), ())), precision=full_precision
    )


def contract_second(left_side, right_side):
    return lax.dot_general(
        left_side, right_side, (((1,), (1,)), ((), ())), precision=full_precision
    )


def butterfly_sum(value, axis):
    levels = lax.axis_size(axis).bit_length() - 1
    for section in range(levels):
        value = value + from_partner(value, axis, section)
    return value


def body(panel_t, trailing, prev_lower_t, prev_upper, leaf_picks, merge_picks):
    slab_rows = panel_t.shape[0]
    rows_here = panel_t.shape[1]
    order = merge_picks.shape[1]
    row_devices = lax.axis_size("rows")
    own_row = lax.axis_index("rows")
    own_column = lax.axis_index("cols")
    leaf_group, leaf_slot = trace_pivots(merge_picks, row_devices)
    owner_mask = leaf_group == own_row
    local_rows = lookup(leaf_picks, jnp.zeros_like(leaf_slot), leaf_slot)
    own_trailing = jnp.take(trailing, local_rows, axis=0)
    own_columns = jnp.take(jnp.concatenate([panel_t, prev_lower_t], 0), local_rows, axis=1)
    own_pivots = jnp.concatenate([own_trailing, own_columns.T], 1)
    own_pivots = jnp.where(owner_mask[:, None], own_pivots, 0.0)
    pivot_data = butterfly_sum(own_pivots.reshape(-1, 128), "rows").reshape(own_pivots.shape)
    pivot_trailing = pivot_data[:, : own_trailing.shape[1]]
    pivot_columns = lax.all_gather(
        pivot_data[:, own_trailing.shape[1] :].T, "cols", axis=0, tiled=False
    )
    block_t = pivot_columns[:, :slab_rows].reshape(order, order)
    prev_pivots = pivot_columns[:, slab_rows:].reshape(order, order)
    middle_pivots = pivot_trailing - contract_first(prev_pivots, prev_upper)
    middle = trailing - contract_first(
        lax.all_gather(prev_lower_t, "cols", axis=0, tiled=True), prev_upper
    )
    panel_full = lax.all_gather(panel_t, "cols", axis=0, tiled=True)
    lower_left, upper_left = factor(block_t.T)
    inverse = upper_inverse(upper_left)
    upper_right = product(unit_lower_inverse(lower_left), middle_pivots)
    lower_full = jnp.dot(inverse.T, panel_full, precision=full_precision)
    lower_tile = lax.dynamic_slice_in_dim(lower_full, own_column * slab_rows, slab_rows, 0)
    updated = middle - contract_first(lower_full, upper_right)
    gram_rows = contract_second(lower_tile, lower_full)
    gram = butterfly_sum(gram_rows, "rows") / (rows_here * row_devices)
    return (lower_tile, upper_left, upper_right, updated, gram)


def solution(mesh):
    return jax.shard_map(
        body,
        mesh=mesh,
        in_specs=(
            P("cols", "rows"),
            P("rows", "cols"),
            P("cols", "rows"),
            P(None, "cols"),
            P("rows", None),
            P(),
        ),
        out_specs=(P("cols", "rows"), P(), P(None, "cols"), P("rows", "cols"), P("cols", None)),
        check_vma=False,
    )
```

```python
import jax
import jax.numpy as jnp
from jax import lax
from jax.experimental import pallas as pl
from jax.experimental.pallas import tpu as pltpu
from jax.sharding import PartitionSpec as P

full_precision = lax.Precision.HIGHEST


def from_partner(shard, axis, apart):
    return lax.ppermute(shard, axis, [(i, i ^ 1 << apart) for i in range(lax.axis_size(axis))])


def lookup(table, group, slot):
    width = table.shape[1]
    slot_hit = slot[:, None] == lax.broadcasted_iota(jnp.int32, (slot.shape[0], width), 1)
    chosen = jnp.zeros((slot.shape[0], width), table.dtype)
    for index in range(table.shape[0]):
        chosen = jnp.where((group == index)[:, None], table[index][None, :], chosen)
    return jnp.sum(jnp.where(slot_hit, chosen, 0), axis=1)


def trace_pivots(merge_picks, row_devices):
    list_width = merge_picks.shape[1]
    leaf_group = jnp.zeros((list_width,), jnp.int32)
    leaf_slot = jnp.arange(list_width, dtype=jnp.int32)
    levels = row_devices.bit_length() - 1
    for section in reversed(range(levels)):
        offset_rows = row_devices - (row_devices >> section)
        groups = 1 << levels - 1 - section
        position = lookup(merge_picks[offset_rows : offset_rows + groups], leaf_group, leaf_slot)
        right_side = (position >= list_width).astype(jnp.int32)
        leaf_group = 2 * leaf_group + right_side
        leaf_slot = position - list_width * right_side
    return (leaf_group, leaf_slot)


def product(left_side, right_side):
    return jnp.dot(left_side, right_side, precision=full_precision)


def unit_lower_inverse(lower):
    order = lower.shape[0]
    identity = jnp.eye(order, dtype=jnp.float32)
    power = identity - lower
    result = identity + power
    covered = 1
    while covered < order - 1:
        power = product(power, power)
        result = product(result, identity + power)
        covered = 2 * covered + 1
    return result


def upper_inverse(upper):
    order = upper.shape[0]
    on_diagonal = lax.broadcasted_iota(jnp.int32, (order, order), 0) == lax.broadcasted_iota(
        jnp.int32, (order, order), 1
    )
    diagonal = jnp.sum(jnp.where(on_diagonal, upper, 0.0), axis=0)
    scaled = upper / diagonal[:, None]
    unit_inverse = unit_lower_inverse(scaled.T).T
    return unit_inverse / diagonal[None, :]


def elimination_kernel(matrix_ref, reduced_ref):
    order = matrix_ref.shape[0]
    reduced_ref[...] = matrix_ref[...]
    phase = 32
    for first_row in range(0, order, phase):
        first_col = (first_row // 128) * 128
        height = order - first_row
        width = order - first_col
        lanes = min(128, width)
        row_index = lax.broadcasted_iota(jnp.int32, (height, 1), 0) + first_row
        col_index = lax.broadcasted_iota(jnp.int32, (1, width), 1) + first_col
        block_index = lax.broadcasted_iota(jnp.int32, (height, lanes), 1) + first_col

        def step(pair, carry):
            first = first_row + 2 * pair
            second = first + 1
            window = reduced_ref[first_row:, first_col:]
            first_line = reduced_ref[pl.ds(first, 1), :][:, first_col:]
            second_line = reduced_ref[pl.ds(second, 1), :][:, first_col:]
            lead = window[:, :lanes]
            on_first = block_index == first
            on_second = block_index == second
            first_column = jnp.sum(jnp.where(on_first, lead, 0.0), axis=1, keepdims=True)
            second_column = jnp.sum(jnp.where(on_second, lead, 0.0), axis=1, keepdims=True)
            first_pivot = jnp.sum(
                jnp.where(col_index == first, first_line, 0.0), axis=1, keepdims=True
            )
            coupling = jnp.sum(
                jnp.where(col_index == second, first_line, 0.0), axis=1, keepdims=True
            )
            second_lead = jnp.sum(
                jnp.where(col_index == first, second_line, 0.0), axis=1, keepdims=True
            )
            below_first = row_index > first
            below_second = row_index > second
            first_factors = jnp.where(below_first, first_column / first_pivot, 0.0)
            first_line = jnp.where(col_index > first, first_line, 0.0)
            second_line = second_line - second_lead / first_pivot * first_line
            second_column = second_column - first_factors * coupling
            second_pivot = jnp.sum(
                jnp.where(col_index == second, second_line, 0.0), axis=1, keepdims=True
            )
            second_factors = jnp.where(below_second, second_column / second_pivot, 0.0)
            second_line = jnp.where(col_index > second, second_line, 0.0)
            window = window - first_factors * first_line - second_factors * second_line
            first_kept = jnp.where(below_first, first_factors, first_column)
            second_kept = jnp.where(below_second, second_factors, second_column)
            reduced_ref[first_row:, first_col:] = window
            reduced_ref[first_row:, first_col : first_col + lanes] = jnp.where(
                on_first, first_kept, jnp.where(on_second, second_kept, window[:, :lanes])
            )
            return carry

        lax.fori_loop(0, min(phase, order - first_row) // 2, step, 0)


def factor(matrix):
    order = matrix.shape[0]
    reduced = pl.pallas_call(
        elimination_kernel,
        out_shape=jax.ShapeDtypeStruct(matrix.shape, matrix.dtype),
    )(matrix)
    lower = jnp.tril(reduced, -1) + jnp.eye(order, dtype=matrix.dtype)
    return (lower, jnp.triu(reduced))


def contract_first(left_side, right_side):
    return lax.dot_general(
        left_side, right_side, (((0,), (0,)), ((), ())), precision=full_precision
    )


def contract_second(left_side, right_side):
    return lax.dot_general(
        left_side, right_side, (((1,), (1,)), ((), ())), precision=full_precision
    )


def butterfly_sum(value, axis):
    levels = lax.axis_size(axis).bit_length() - 1
    for section in range(levels):
        value = value + from_partner(value, axis, section)
    return value


def body(panel_t, trailing, prev_lower_t, prev_upper, leaf_picks, merge_picks):
    slab_rows = panel_t.shape[0]
    rows_here = panel_t.shape[1]
    order = merge_picks.shape[1]
    row_devices = lax.axis_size("rows")
    own_row = lax.axis_index("rows")
    own_column = lax.axis_index("cols")
    leaf_group, leaf_slot = trace_pivots(merge_picks, row_devices)
    owner_mask = leaf_group == own_row
    local_rows = lookup(leaf_picks, jnp.zeros_like(leaf_slot), leaf_slot)
    own_trailing = jnp.take(trailing, local_rows, axis=0)
    own_columns = jnp.concatenate(
        [jnp.take(panel_t, local_rows, axis=1), jnp.take(prev_lower_t, local_rows, axis=1)], 0
    )
    own_pivots = jnp.concatenate([own_trailing, own_columns.T], 1)
    own_pivots = jnp.where(owner_mask[:, None], own_pivots, 0.0)
    pivot_data = butterfly_sum(own_pivots.reshape(-1, 128), "rows").reshape(own_pivots.shape)
    pivot_trailing = pivot_data[:, : own_trailing.shape[1]]
    pivot_columns = lax.all_gather(
        pivot_data[:, own_trailing.shape[1] :].T, "cols", axis=0, tiled=False
    )
    block_t = pivot_columns[:, :slab_rows].reshape(order, order)
    prev_pivots = pivot_columns[:, slab_rows:].reshape(order, order)
    middle_pivots = pivot_trailing - contract_first(prev_pivots, prev_upper)
    middle = trailing - contract_first(
        lax.all_gather(prev_lower_t, "cols", axis=0, tiled=True), prev_upper
    )
    panel_full = lax.all_gather(panel_t, "cols", axis=0, tiled=True)
    lower_left, upper_left = factor(block_t.T)
    inverse = upper_inverse(upper_left)
    upper_right = product(unit_lower_inverse(lower_left), middle_pivots)
    lower_full = jnp.dot(inverse.T, panel_full, precision=full_precision)
    lower_tile = lax.dynamic_slice_in_dim(lower_full, own_column * slab_rows, slab_rows, 0)
    updated = middle - contract_first(lower_full, upper_right)
    gram_rows = contract_second(lower_tile, lower_full)
    gram = butterfly_sum(gram_rows, "rows") / (rows_here * row_devices)
    return (lower_tile, upper_left, upper_right, updated, gram)


def solution(mesh):
    return jax.shard_map(
        body,
        mesh=mesh,
        in_specs=(
            P("cols", "rows"),
            P("rows", "cols"),
            P("cols", "rows"),
            P(None, "cols"),
            P("rows", None),
            P(),
        ),
        out_specs=(P("cols", "rows"), P(), P(None, "cols"), P("rows", "cols"), P("cols", None)),
        check_vma=False,
    )
```
